512 devices in a mesh: dp: 32 (over y, z_hi, x), tensor: 16 (over z_lo, core).
Axes of the slice: x: 4, y: 4, z: 16 (z_hi: 2, z_lo: 8; z = z_hi * 8 + z_lo), core: 2. Of those that a mesh axis runs over, the one named last changes fastest.
Arguments:
- inner_x: bfloat16 [32768, 8192], P(('dp', 'tensor')), parts along dimension 0, may hold values from -6 to 6
- inner_bc: bfloat16 [32768, 2048], P(('dp', 'tensor')), parts along dimension 0, may hold values from -6 to 6
- step_raw: bfloat16 [32768, 128], P(('dp', 'tensor')), parts along dimension 0, may hold values from -5 to 5
- conv_state_x: bfloat16 [96, 8192], P('dp', 'tensor'), parts along dimension 0, may hold values from -6 to 6
- conv_state_bc: bfloat16 [96, 2048], P('dp'), parts along dimension 0, may hold values from -6 to 6
- conv_weight_x: bfloat16 [4, 8192], P(None, 'tensor'), may hold values from -3 to 3
- conv_bias_x: bfloat16 [8192], P('tensor'), may hold values from -3 to 3
- conv_weight_bc: bfloat16 [4, 2048], replicated, may hold values from -3 to 3
- conv_bias_bc: bfloat16 [2048], replicated, may hold values from -3 to 3
- step_bias: float32 [128], P('tensor'), may hold values from -4 to -2
- decay_rate: float32 [128], P('tensor'), may hold values from 0 to 1, as said below
- skip_gain: float32 [128], P('tensor'), may hold values from 0.5 to 1.5
- norm_weight: bfloat16 [8192], replicated, may hold values from 0.5 to 1.5
- scan_state: float32 [4096, 64, 256], P(('dp', 'tensor')), parts along dimension 0, may hold values from -3 to 3
Outputs:
- normed: bfloat16 [32768, 8192], P(('dp', 'tensor')), parts along dimension 0
- final_state: float32 [4096, 64, 256], P(('dp', 'tensor')), parts along dimension 0
- conv_tail_x: bfloat16 [96, 8192], P('dp', 'tensor'), parts along dimension 0
- conv_tail_bc: bfloat16 [96, 2048], P('dp', 'tensor'), parts along dimension 0
The draws below stay inside these ranges and needn't reach their ends.
There are 32 independent parts, one for each index of `dp`. The reference program is written for one: setup_inputs(seed, part) draws one part's arguments, and reference() takes and returns one part's arrays. A program takes and returns all parts, laid end to end along the dimension named above; an argument that names none is the same for every part. Nothing has to cross between parts.
Inputs may be any that keep to these rules, and one draw needn't show every extreme that they name: decay_rate lies between 2 / 1024 and 1 / 2.
All inputs are finite; a program needn't handle non-finite values.
Results may differ from the reference program's by a relative error of at most 0.0051.
Values may be sent and summed in bfloat16 or wider, within the bound.
No kernel may reach another device: no remote copies, remote signals or barrier semaphores. Data moves between devices by JAX's collectives and lax.ppermute only.
A program may use at most 64 MiB of HBM per device.

```python
import math
import jax
import jax.numpy as jnp
from jax import lax

HEADS = 128
HEAD_DIM = 64
STATE = 256
GROUPS = 4
CONV_K = 4
TOKENS = 1024
INNER = 8192


def draw_decay_rate(key, part):
    lower = math.log(2.0 / TOKENS)
    upper = math.log(0.5)
    unit = jax.random.uniform(key, (HEADS,), jnp.float32)
    return jnp.exp(lower + (upper - lower) * unit).astype(jnp.float32)


def block_levels(key, extent, cuts, smallest, top_value):
    level = 1.0
    for position, shards_of in cuts:
        steps = jax.random.uniform(jax.random.fold_in(jax.random.fold_in(key, 6), position), (shards_of,), jnp.float32, smallest / len(cuts), top_value / len(cuts))
        level = level * jnp.repeat(jnp.exp(steps), extent[position] // shards_of).reshape((-1,) + (1,) * (len(extent) - 1 - position))
    return level


def normal_values(key, dims, scale, reach, shards=(), kind=jnp.bfloat16):
    entries = scale * jax.random.normal(key, dims, jnp.float32)
    if shards:
        entries = entries * block_levels(key, dims, shards, -0.22, 0.18)
    return jnp.clip(entries, -reach, reach).astype(kind)


def setup_inputs(seed: int = 0, part: int = 0) -> dict:
    keys = jax.random.split(jax.random.key(seed), 15)
    part_keys = jax.random.split(jax.random.fold_in(keys[14], part), 15)
    return {
        "inner_x": normal_values(part_keys[0], (TOKENS, INNER), 1.0, 6.0, ((0, 16),)),
        "inner_bc": normal_values(part_keys[1], (TOKENS, 2 * GROUPS * STATE), 1.0, 6.0, ((0, 16),)),
        "step_raw": normal_values(part_keys[2], (TOKENS, HEADS), 1.0, 5.0, ((0, 16),)),
        "conv_state_x": normal_values(part_keys[3], (CONV_K - 1, INNER), 1.0, 6.0, ((1, 16),)),
        "conv_state_bc": normal_values(part_keys[4], (CONV_K - 1, 2 * GROUPS * STATE), 1.0, 6.0),
        "conv_weight_x": normal_values(keys[5], (CONV_K, INNER), CONV_K ** -0.5, 3.0, ((1, 16),)),
        "conv_bias_x": normal_values(keys[6], (INNER,), 0.5, 3.0, ((0, 16),)),
        "conv_weight_bc": normal_values(keys[7], (CONV_K, 2 * GROUPS * STATE), CONV_K ** -0.5, 3.0),
        "conv_bias_bc": normal_values(keys[8], (2 * GROUPS * STATE,), 0.5, 3.0),
        "step_bias": jnp.clip(-4.0 + 2.0 * jax.random.uniform(keys[9], (HEADS,), jnp.float32) ** block_levels(keys[9], (HEADS,), ((0, 16),), -0.2, 0.2), -4.0, -2.0),
        "decay_rate": draw_decay_rate(jax.random.fold_in(keys[14], 71), part),
        "skip_gain": jnp.clip(0.5 + 1.0 * jax.random.uniform(keys[11], (HEADS,), jnp.float32) ** block_levels(keys[11], (HEADS,), ((0, 16),), -0.2, 0.2), 0.5, 1.5),
        "norm_weight": jnp.clip(1.0 + 0.1 * jax.random.normal(keys[12], (INNER,), jnp.float32), 0.5, 1.5).astype(jnp.bfloat16),
        "scan_state": normal_values(part_keys[13], (HEADS, HEAD_DIM, STATE), 0.3, 3.0, ((0, 16),), jnp.float32),
    }


EPSILON = 1e-05

def causal_conv(raw, state, weight, bias):
    length = raw.shape[0]
    padded = jnp.concatenate([state.astype(jnp.float32), raw.astype(jnp.float32)], axis=0)
    total = jnp.zeros(raw.shape, jnp.float32) + bias.astype(jnp.float32)[None, :]
    for kernel_tap in range(CONV_K):
        total = total + weight[kernel_tap].astype(jnp.float32)[None, :] * padded[kernel_tap:kernel_tap + length]
    return jax.nn.silu(total).astype(jnp.bfloat16)

def state_mix(mixed_x, mixed_bc, step_raw, step_bias, decay_rate, skip_gain, scan_state, groups_here):
    length = mixed_x.shape[0]
    heads_here = step_raw.shape[1]
    per_group = heads_here // groups_here
    step_size = jax.nn.softplus(step_raw.astype(jnp.float32) + step_bias[None, :])
    running = jnp.cumsum(-step_size * decay_rate[None, :], axis=0)
    halves = mixed_bc.reshape(length, groups_here, 2, STATE)
    input_map = halves[:, :, 0, :]
    output_map = halves[:, :, 1, :]
    step_cols = jnp.transpose(step_size)
    running_cols = jnp.transpose(running)
    query_rows = min(512, length)
    pieces = []
    for row_start in range(0, length, query_rows):
        row_stop = row_start + query_rows
        scores = jnp.einsum('tgn,sgn->gts', output_map[row_start:row_stop].astype(jnp.float32), input_map[:row_stop].astype(jnp.float32), precision=lax.Precision.HIGHEST)
        causal = row_start + lax.broadcasted_iota(jnp.int32, (query_rows, row_stop), 0) >= lax.broadcasted_iota(jnp.int32, (query_rows, row_stop), 1)
        visible = mixed_x[:row_stop]

        def one_head(item, scores=scores, causal=causal, visible=visible, row_start=row_start, row_stop=row_stop):
            head_index, step_head, running_head = item
            group_scores = lax.dynamic_index_in_dim(scores, head_index // per_group, 0, keepdims=False)
            log_gap = running_head[row_start:row_stop, None] - running_head[None, :row_stop]
            decayed = jnp.exp(jnp.where(causal, log_gap, 0.0))
            weights = jnp.where(causal, group_scores * decayed * step_head[None, :row_stop], 0.0).astype(jnp.bfloat16)
            values = lax.dynamic_slice_in_dim(visible, head_index * HEAD_DIM, HEAD_DIM, 1)
            return jnp.dot(weights, values, preferred_element_type=jnp.float32)
        local_mix = lax.map(one_head, (jnp.arange(heads_here, dtype=jnp.int32), step_cols, running_cols))
        pieces.append(jnp.transpose(local_mix, (1, 0, 2)).reshape(query_rows, heads_here * HEAD_DIM))
    local_all = jnp.concatenate(pieces, axis=0)
    grouped_state = scan_state.reshape(groups_here, per_group, HEAD_DIM, STATE)
    carried = jnp.einsum('tgn,ghpn->tghp', output_map.astype(jnp.float32), grouped_state, precision=lax.Precision.HIGHEST)
    carried = carried.reshape(length, heads_here, HEAD_DIM) * jnp.exp(running)[:, :, None]
    channels = mixed_x.reshape(length, heads_here, HEAD_DIM).astype(jnp.float32)
    mixed = local_all.reshape(length, heads_here, HEAD_DIM) + carried + skip_gain[None, :, None] * channels
    mixed_y = mixed.reshape(length, heads_here * HEAD_DIM).astype(jnp.bfloat16)
    tail_decay = jnp.exp(running[length - 1][None, :] - running) * step_size
    weighted = (input_map.astype(jnp.float32)[:, :, None, :] * tail_decay.reshape(length, groups_here, per_group)[:, :, :, None]).astype(jnp.bfloat16)
    gathered_in = jnp.einsum('tghp,tghn->ghpn', mixed_x.reshape(length, groups_here, per_group, HEAD_DIM).astype(jnp.float32), weighted.astype(jnp.float32), precision=lax.Precision.HIGHEST)
    final = jnp.exp(running[length - 1]).reshape(groups_here, per_group)[:, :, None, None] * grouped_state + gathered_in
    return (mixed_y, final.reshape(heads_here, HEAD_DIM, STATE))

def group_norm(mixed_y, norm_weight):
    rows = mixed_y.shape[0]
    values = mixed_y.astype(jnp.float32).reshape(rows, GROUPS, INNER // GROUPS)
    mean_square = lax.optimization_barrier(jnp.mean(values * values, axis=2, keepdims=True))
    scaled = (values * lax.rsqrt(mean_square + EPSILON)).reshape(rows, INNER)
    return (scaled * norm_weight.astype(jnp.float32)[None, :]).astype(jnp.bfloat16)

def reference(inner_x, inner_bc, step_raw, conv_state_x, conv_state_bc, conv_weight_x, conv_bias_x, conv_weight_bc, conv_bias_bc, step_bias, decay_rate, skip_gain, norm_weight, scan_state):
    mixed_x = causal_conv(inner_x, conv_state_x, conv_weight_x, conv_bias_x)
    mixed_bc = causal_conv(inner_bc, conv_state_bc, conv_weight_bc, conv_bias_bc)
    mixed_y, final_state = state_mix(mixed_x, mixed_bc, step_raw, step_bias, decay_rate, skip_gain, scan_state, GROUPS)
    normed = group_norm(mixed_y, norm_weight)
    return (normed, final_state, inner_x[TOKENS - CONV_K + 1:], inner_bc[TOKENS - CONV_K + 1:])
```

```python
import functools

import jax
import jax.numpy as jnp
from jax import lax
import numpy as np
from jax.sharding import Mesh, PartitionSpec as P

HEAD_DIM = 64
STATE = 256
GROUPS = 4
CONV_K = 4
INNER = 8192


EPSILON = 1e-05
TENSOR = ("tg", "tj")


def causal_conv(raw, state, weight, bias):
    length = raw.shape[0]
    padded = jnp.concatenate([state.astype(jnp.float32), raw.astype(jnp.float32)], axis=0)
    total = jnp.zeros(raw.shape, jnp.float32) + bias.astype(jnp.float32)[None, :]
    for kernel_tap in range(CONV_K):
        total = (
            total
            + weight[kernel_tap].astype(jnp.float32)[None, :]
            * padded[kernel_tap : kernel_tap + length]
        )
    return jax.nn.silu(total).astype(jnp.bfloat16)


def state_mix(
    mixed_x, mixed_bc, step_raw, step_bias, decay_rate, skip_gain, scan_state, groups_here
):
    length = mixed_x.shape[0]
    heads_here = step_raw.shape[1]
    per_group = heads_here // groups_here
    step_size = jax.nn.softplus(step_raw.astype(jnp.float32) + step_bias[None, :])
    running = jnp.cumsum(-step_size * decay_rate[None, :], axis=0)
    halves = mixed_bc.reshape(length, groups_here, 2, STATE)
    input_map = halves[:, :, 0, :]
    output_map = halves[:, :, 1, :]
    step_cols = jnp.transpose(step_size)
    running_cols = jnp.transpose(running)
    query_rows = min(512, length)
    pieces = []
    for row_start in range(0, length, query_rows):
        row_stop = row_start + query_rows
        scores = jnp.einsum(
            "tgn,sgn->gts",
            output_map[row_start:row_stop],
            input_map[:row_stop],
            preferred_element_type=jnp.float32,
        )
        causal = row_start + lax.broadcasted_iota(
            jnp.int32, (query_rows, row_stop), 0
        ) >= lax.broadcasted_iota(jnp.int32, (query_rows, row_stop), 1)
        visible = mixed_x[:row_stop]

        def one_head(
            item,
            scores=scores,
            causal=causal,
            visible=visible,
            row_start=row_start,
            row_stop=row_stop,
        ):
            head_index, step_head, running_head = item
            group_scores = lax.dynamic_index_in_dim(
                scores, head_index // per_group, 0, keepdims=False
            )
            log_gap = running_head[row_start:row_stop, None] - running_head[None, :row_stop]
            decayed = jnp.exp(jnp.where(causal, log_gap, 0.0))
            weights = jnp.where(
                causal, group_scores * decayed * step_head[None, :row_stop], 0.0
            ).astype(jnp.bfloat16)
            values = lax.dynamic_slice_in_dim(visible, head_index * HEAD_DIM, HEAD_DIM, 1)
            return jnp.dot(weights, values, preferred_element_type=jnp.float32)

        local_mix = lax.map(
            one_head, (jnp.arange(heads_here, dtype=jnp.int32), step_cols, running_cols)
        )
        pieces.append(
            jnp.transpose(local_mix, (1, 0, 2)).reshape(query_rows, heads_here * HEAD_DIM)
        )
    local_all = jnp.concatenate(pieces, axis=0)
    grouped_state = scan_state.reshape(groups_here, per_group, HEAD_DIM, STATE)
    carried = jnp.einsum(
        "tgn,ghpn->tghp",
        output_map.astype(jnp.float32),
        grouped_state,
        precision=lax.Precision.HIGHEST,
    )
    carried = carried.reshape(length, heads_here, HEAD_DIM) * jnp.exp(running)[:, :, None]
    channels = mixed_x.reshape(length, heads_here, HEAD_DIM).astype(jnp.float32)
    mixed = (
        local_all.reshape(length, heads_here, HEAD_DIM)
        + carried
        + skip_gain[None, :, None] * channels
    )
    mixed_y = mixed.reshape(length, heads_here * HEAD_DIM).astype(jnp.bfloat16)
    tail_decay = jnp.exp(running[length - 1][None, :] - running) * step_size
    weighted = (
        input_map.astype(jnp.float32)[:, :, None, :]
        * tail_decay.reshape(length, groups_here, per_group)[:, :, :, None]
    ).astype(jnp.bfloat16)
    gathered_in = jnp.einsum(
        "tghp,tghn->ghpn",
        mixed_x.reshape(length, groups_here, per_group, HEAD_DIM),
        weighted,
        preferred_element_type=jnp.float32,
    )
    final = (
        jnp.exp(running[length - 1]).reshape(groups_here, per_group)[:, :, None, None]
        * grouped_state
        + gathered_in
    )
    return (mixed_y, final.reshape(heads_here, HEAD_DIM, STATE))


def group_norm(mixed_y, norm_weight):
    rows = mixed_y.shape[0]
    values = mixed_y.astype(jnp.float32).reshape(rows, GROUPS, INNER // GROUPS)
    mean_square = jnp.mean(values * values, axis=2, keepdims=True)
    scaled = (values * lax.rsqrt(mean_square + EPSILON)).reshape(rows, INNER)
    return (scaled * norm_weight.astype(jnp.float32)[None, :]).astype(jnp.bfloat16)


def local(
    inner_x,
    inner_bc,
    step_raw,
    conv_state_x,
    conv_state_bc,
    conv_weight_x,
    conv_bias_x,
    conv_weight_bc,
    conv_bias_bc,
    step_bias,
    decay_rate,
    skip_gain,
    norm_weight,
    scan_state,
    *,
    group_size,
    tensor_count,
):
    device_rank = lax.axis_index("tg") * group_size + lax.axis_index("tj")
    token_rows = inner_x.shape[0]
    heads_here = step_bias.shape[0]
    x_width = heads_here * HEAD_DIM
    bc_width = inner_bc.shape[1] // tensor_count
    x_send = jnp.transpose(inner_x.reshape(token_rows, tensor_count, x_width), (1, 0, 2))
    bc_send = jnp.transpose(inner_bc.reshape(token_rows, tensor_count, bc_width), (1, 0, 2))
    step_send = jnp.transpose(step_raw.reshape(token_rows, tensor_count, heads_here), (1, 0, 2))
    send = jnp.concatenate(
        [
            x_send.reshape(tensor_count, -1),
            bc_send.reshape(tensor_count, -1),
            step_send.reshape(tensor_count, -1),
        ],
        axis=1,
    )
    recv = lax.all_to_all(send, TENSOR, 0, 0, tiled=True)
    length = tensor_count * token_rows
    x_end = token_rows * x_width
    bc_end = x_end + token_rows * bc_width
    head_x = recv[:, :x_end].reshape(length, x_width)
    head_bc_part = recv[:, x_end:bc_end].reshape(length, bc_width)
    head_step = recv[:, bc_end:].reshape(length, heads_here)
    column_start = device_rank * bc_width
    own_state_bc = lax.dynamic_slice_in_dim(conv_state_bc, column_start, bc_width, 1)
    own_weight_bc = lax.dynamic_slice_in_dim(conv_weight_bc, column_start, bc_width, 1)
    own_bias_bc = lax.dynamic_slice_in_dim(conv_bias_bc, column_start, bc_width, 0)
    mixed_bc_part = causal_conv(head_bc_part, own_state_bc, own_weight_bc, own_bias_bc)
    mixed_bc = lax.all_gather(mixed_bc_part, "tj", axis=1, tiled=True)
    mixed_x = causal_conv(head_x, conv_state_x, conv_weight_x, conv_bias_x)
    mixed_y, final_state = state_mix(
        mixed_x, mixed_bc, head_step, step_bias, decay_rate, skip_gain, scan_state, 1
    )
    token_y = lax.all_to_all(mixed_y, TENSOR, split_axis=0, concat_axis=1, tiled=True)
    normed = group_norm(token_y, norm_weight)
    tail_x = head_x[length - CONV_K + 1 :]
    tail_bc = head_bc_part[length - CONV_K + 1 :]
    return (normed, final_state, tail_x, tail_bc)


def solution(mesh):
    dp_count = mesh.shape["dp"]
    tensor_count = mesh.shape["tensor"]
    group_size = tensor_count // GROUPS
    grouped = Mesh(
        np.asarray(mesh.devices).reshape(dp_count, GROUPS, group_size), ("dp", "tg", "tj")
    )
    rows = ("dp",) + TENSOR
    return jax.shard_map(
        functools.partial(local, group_size=group_size, tensor_count=tensor_count),
        mesh=grouped,
        in_specs=(
            P(rows, None),
            P(rows, None),
            P(rows, None),
            P("dp", TENSOR),
            P("dp", None),
            P(None, TENSOR),
            P(TENSOR),
            P(),
            P(),
            P(TENSOR),
            P(TENSOR),
            P(TENSOR),
            P(),
            P(rows, None, None),
        ),
        out_specs=(
            P(rows, None),
            P(rows, None, None),
            P("dp", TENSOR),
            P("dp", TENSOR),
        ),
        check_vma=False,
    )
```

```python
import functools

import jax
import jax.numpy as jnp
from jax import lax
import numpy as np
from jax.sharding import Mesh, PartitionSpec as P

HEAD_DIM = 64
STATE = 256
GROUPS = 4
CONV_K = 4
INNER = 8192


EPSILON = 1e-05
TENSOR = ("tg", "tj")


def causal_conv(raw, state, weight, bias):
    length = raw.shape[0]
    padded = jnp.concatenate([state.astype(jnp.float32), raw.astype(jnp.float32)], axis=0)
    total = jnp.zeros(raw.shape, jnp.float32) + bias.astype(jnp.float32)[None, :]
    for kernel_tap in range(CONV_K):
        total = (
            total
            + weight[kernel_tap].astype(jnp.float32)[None, :]
            * padded[kernel_tap : kernel_tap + length]
        )
    return jax.nn.silu(total).astype(jnp.bfloat16)


def group_norm(mixed_y, norm_weight):
    rows = mixed_y.shape[0]
    values = mixed_y.astype(jnp.float32).reshape(rows, GROUPS, INNER // GROUPS)
    mean_square = jnp.mean(values * values, axis=2, keepdims=True)
    scaled = (values * lax.rsqrt(mean_square + EPSILON)).reshape(rows, INNER)
    return (scaled * norm_weight.astype(jnp.float32)[None, :]).astype(jnp.bfloat16)


def local(
    inner_x,
    inner_bc,
    step_raw,
    conv_state_x,
    conv_state_bc,
    conv_weight_x,
    conv_bias_x,
    conv_weight_bc,
    conv_bias_bc,
    step_bias,
    decay_rate,
    skip_gain,
    norm_weight,
    scan_state,
    *,
    group_size,
    tensor_count,
):
    device_rank = lax.axis_index("tg") * group_size + lax.axis_index("tj")
    token_rows = inner_x.shape[0]
    heads_here = step_bias.shape[0]
    x_width = heads_here * HEAD_DIM
    bc_width = inner_bc.shape[1] // tensor_count
    length = tensor_count * token_rows

    bc_send = jnp.transpose(inner_bc.reshape(token_rows, tensor_count, bc_width), (1, 0, 2))
    step_send = jnp.transpose(step_raw.reshape(token_rows, tensor_count, heads_here), (1, 0, 2))
    small_send = jnp.concatenate(
        [bc_send.reshape(tensor_count, -1), step_send.reshape(tensor_count, -1)], axis=1
    )
    small_recv = lax.all_to_all(small_send, TENSOR, 0, 0, tiled=True)
    bc_end = token_rows * bc_width
    head_bc_part = small_recv[:, :bc_end].reshape(length, bc_width)
    head_step = small_recv[:, bc_end:].reshape(length, heads_here)

    x_send = jnp.transpose(inner_x.reshape(token_rows, tensor_count, x_width), (1, 0, 2))
    x_recv = lax.all_to_all(x_send, TENSOR, 0, 0, tiled=True)
    head_x = x_recv.reshape(length, x_width)

    column_start = device_rank * bc_width
    own_state_bc = lax.dynamic_slice_in_dim(conv_state_bc, column_start, bc_width, 1)
    own_weight_bc = lax.dynamic_slice_in_dim(conv_weight_bc, column_start, bc_width, 1)
    own_bias_bc = lax.dynamic_slice_in_dim(conv_bias_bc, column_start, bc_width, 0)
    mixed_bc_part = causal_conv(head_bc_part, own_state_bc, own_weight_bc, own_bias_bc)
    mixed_bc = lax.all_gather(mixed_bc_part, "tj", axis=1, tiled=True)
    input_map = mixed_bc[:, :STATE]
    output_map = mixed_bc[:, STATE:]

    step_size = jax.nn.softplus(head_step.astype(jnp.float32) + step_bias[None, :])
    running = jnp.cumsum(-step_size * decay_rate[None, :], axis=0)
    step_cols = jnp.transpose(step_size)
    running_cols = jnp.transpose(running)

    mixed_x = causal_conv(head_x, conv_state_x, conv_weight_x, conv_bias_x)
    values = mixed_x.reshape(length, heads_here, HEAD_DIM)

    query_rows = min(256, length)
    pieces = []
    for row_start in range(0, length, query_rows):
        row_stop = row_start + query_rows
        scores = jnp.einsum(
            "tn,sn->ts",
            output_map[row_start:row_stop],
            input_map[:row_stop],
            preferred_element_type=jnp.float32,
        )
        causal = row_start + lax.broadcasted_iota(
            jnp.int32, (query_rows, row_stop), 0
        ) >= lax.broadcasted_iota(jnp.int32, (query_rows, row_stop), 1)
        log_gap = running_cols[:, row_start:row_stop, None] - running_cols[:, None, :row_stop]
        decayed = jnp.exp(jnp.where(causal[None], log_gap, 0.0))
        weights = jnp.where(
            causal[None], scores[None] * decayed * step_cols[:, None, :row_stop], 0.0
        ).astype(jnp.bfloat16)
        weights = lax.optimization_barrier(weights)
        pieces.append(
            jnp.einsum(
                "hts,shp->thp", weights, values[:row_stop], preferred_element_type=jnp.float32
            )
        )
    local_all = jnp.concatenate(pieces, axis=0)
    carried = jnp.einsum(
        "tn,hpn->thp",
        output_map.astype(jnp.float32),
        scan_state,
        precision=lax.Precision.HIGHEST,
    )
    carried = carried * jnp.exp(running)[:, :, None]
    channels = values.astype(jnp.float32)
    mixed = local_all + carried + skip_gain[None, :, None] * channels
    mixed_y = mixed.reshape(length, x_width).astype(jnp.bfloat16)
    tail_decay = jnp.exp(running[length - 1][None, :] - running) * step_size
    weighted = (input_map.astype(jnp.float32)[:, None, :] * tail_decay[:, :, None]).astype(
        jnp.bfloat16
    )
    gathered_in = jnp.einsum(
        "shp,shn->hpn", values, weighted, preferred_element_type=jnp.float32
    )
    final_state = jnp.exp(running[length - 1])[:, None, None] * scan_state + gathered_in

    token_y = lax.all_to_all(mixed_y, TENSOR, split_axis=0, concat_axis=1, tiled=True)
    normed = group_norm(token_y, norm_weight)
    tail_x = head_x[length - CONV_K + 1 :]
    tail_bc = head_bc_part[length - CONV_K + 1 :]
    return (normed, final_state, tail_x, tail_bc)


def solution(mesh):
    dp_count = mesh.shape["dp"]
    tensor_count = mesh.shape["tensor"]
    group_size = tensor_count // GROUPS
    grouped = Mesh(
        np.asarray(mesh.devices).reshape(dp_count, GROUPS, group_size), ("dp", "tg", "tj")
    )
    rows = ("dp",) + TENSOR
    return jax.shard_map(
        functools.partial(local, group_size=group_size, tensor_count=tensor_count),
        mesh=grouped,
        in_specs=(
            P(rows, None),
            P(rows, None),
            P(rows, None),
            P("dp", TENSOR),
            P("dp", None),
            P(None, TENSOR),
            P(TENSOR),
            P(),
            P(),
            P(TENSOR),
            P(TENSOR),
            P(TENSOR),
            P(),
            P(rows, None, None),
        ),
        out_specs=(
            P(rows, None),
            P(rows, None, None),
            P("dp", TENSOR),
            P("dp", TENSOR),
        ),
        check_vma=False,
    )
```

```python
import functools

import jax
import jax.numpy as jnp
from jax import lax
import numpy as np
from jax.sharding import Mesh, PartitionSpec as P

HEAD_DIM = 64
STATE = 256
GROUPS = 4
CONV_K = 4
INNER = 8192


EPSILON = 1e-05
TENSOR = ("tg", "tj")


def causal_conv(raw, state, weight, bias):
    length = raw.shape[0]
    padded = jnp.concatenate([state.astype(jnp.float32), raw.astype(jnp.float32)], axis=0)
    total = jnp.zeros(raw.shape, jnp.float32) + bias.astype(jnp.float32)[None, :]
    for kernel_tap in range(CONV_K):
        total = (
            total
            + weight[kernel_tap].astype(jnp.float32)[None, :]
            * padded[kernel_tap : kernel_tap + length]
        )
    return jax.nn.silu(total).astype(jnp.bfloat16)


def group_norm(mixed_y, norm_weight):
    rows = mixed_y.shape[0]
    values = mixed_y.astype(jnp.float32).reshape(rows, GROUPS, INNER // GROUPS)
    mean_square = jnp.mean(values * values, axis=2, keepdims=True)
    scaled = (values * lax.rsqrt(mean_square + EPSILON)).reshape(rows, INNER)
    return (scaled * norm_weight.astype(jnp.float32)[None, :]).astype(jnp.bfloat16)


def local(
    inner_x,
    inner_bc,
    step_raw,
    conv_state_x,
    conv_state_bc,
    conv_weight_x,
    conv_bias_x,
    conv_weight_bc,
    conv_bias_bc,
    step_bias,
    decay_rate,
    skip_gain,
    norm_weight,
    scan_state,
    *,
    group_size,
    tensor_count,
):
    device_rank = lax.axis_index("tg") * group_size + lax.axis_index("tj")
    token_rows = inner_x.shape[0]
    heads_here = step_bias.shape[0]
    x_width = heads_here * HEAD_DIM
    bc_width = inner_bc.shape[1] // tensor_count
    length = tensor_count * token_rows

    bc_send = jnp.transpose(inner_bc.reshape(token_rows, tensor_count, bc_width), (1, 0, 2))
    step_send = jnp.transpose(step_raw.reshape(token_rows, tensor_count, heads_here), (1, 0, 2))
    small_send = jnp.concatenate(
        [bc_send.reshape(tensor_count, -1), step_send.reshape(tensor_count, -1)], axis=1
    )
    small_recv = lax.all_to_all(small_send, TENSOR, 0, 0, tiled=True)
    bc_end = token_rows * bc_width
    head_bc_part = small_recv[:, :bc_end].reshape(length, bc_width)
    head_step = small_recv[:, bc_end:].reshape(length, heads_here)

    x_send = jnp.transpose(inner_x.reshape(token_rows, tensor_count, x_width), (1, 0, 2))
    x_recv = lax.all_to_all(x_send, TENSOR, 0, 0, tiled=True)
    head_x = x_recv.reshape(length, x_width)

    column_start = device_rank * bc_width
    own_state_bc = lax.dynamic_slice_in_dim(conv_state_bc, column_start, bc_width, 1)
    own_weight_bc = lax.dynamic_slice_in_dim(conv_weight_bc, column_start, bc_width, 1)
    own_bias_bc = lax.dynamic_slice_in_dim(conv_bias_bc, column_start, bc_width, 0)
    mixed_bc_part = causal_conv(head_bc_part, own_state_bc, own_weight_bc, own_bias_bc)
    group_rank = lax.axis_index("tj")
    slabs = [mixed_bc_part]
    for shift in range(1, group_size):
        slabs.append(
            lax.ppermute(
                mixed_bc_part,
                "tj",
                [(source, (source + shift) % group_size) for source in range(group_size)],
            )
        )
    stacked = jnp.stack(slabs)
    order = (group_rank - jnp.arange(group_size, dtype=jnp.int32)) % group_size
    ordered = jnp.take(stacked, order, axis=0)
    mixed_bc = jnp.transpose(ordered, (1, 0, 2)).reshape(length, group_size * bc_width)
    input_map = mixed_bc[:, :STATE]
    output_map = mixed_bc[:, STATE:]

    step_size = jax.nn.softplus(head_step.astype(jnp.float32) + step_bias[None, :])
    running = jnp.cumsum(-step_size * decay_rate[None, :], axis=0)
    step_cols = jnp.transpose(step_size)
    running_cols = jnp.transpose(running)

    mixed_x = causal_conv(head_x, conv_state_x, conv_weight_x, conv_bias_x)
    values = mixed_x.reshape(length, heads_here, HEAD_DIM)

    query_rows = min(256, length)
    pieces = []
    for row_start in range(0, length, query_rows):
        row_stop = row_start + query_rows
        scores = jnp.einsum(
            "tn,sn->ts",
            output_map[row_start:row_stop],
            input_map[:row_stop],
            preferred_element_type=jnp.float32,
        )
        causal = row_start + lax.broadcasted_iota(
            jnp.int32, (query_rows, row_stop), 0
        ) >= lax.broadcasted_iota(jnp.int32, (query_rows, row_stop), 1)
        log_gap = running_cols[:, row_start:row_stop, None] - running_cols[:, None, :row_stop]
        decayed = jnp.exp(jnp.where(causal[None], log_gap, 0.0))
        weights = jnp.where(
            causal[None], scores[None] * decayed * step_cols[:, None, :row_stop], 0.0
        ).astype(jnp.bfloat16)
        weights = lax.optimization_barrier(weights)
        pieces.append(
            jnp.einsum(
                "hts,shp->thp", weights, values[:row_stop], preferred_element_type=jnp.float32
            )
        )
    local_all = jnp.concatenate(pieces, axis=0)
    carried = jnp.einsum(
        "tn,hpn->thp",
        output_map.astype(jnp.float32),
        scan_state,
        precision=lax.Precision.HIGHEST,
    )
    carried = carried * jnp.exp(running)[:, :, None]
    channels = values.astype(jnp.float32)
    mixed = local_all + carried + skip_gain[None, :, None] * channels
    mixed_y = mixed.reshape(length, x_width).astype(jnp.bfloat16)
    tail_decay = jnp.exp(running[length - 1][None, :] - running) * step_size
    weighted = (input_map.astype(jnp.float32)[:, None, :] * tail_decay[:, :, None]).astype(
        jnp.bfloat16
    )
    gathered_in = jnp.einsum(
        "shp,shn->hpn", values, weighted, preferred_element_type=jnp.float32
    )
    final_state = jnp.exp(running[length - 1])[:, None, None] * scan_state + gathered_in

    token_y = lax.all_to_all(mixed_y, TENSOR, split_axis=0, concat_axis=1, tiled=True)
    normed = group_norm(token_y, norm_weight)
    tail_x = head_x[length - CONV_K + 1 :]
    tail_bc = head_bc_part[length - CONV_K + 1 :]
    return (normed, final_state, tail_x, tail_bc)


def solution(mesh):
    dp_count = mesh.shape["dp"]
    tensor_count = mesh.shape["tensor"]
    group_size = tensor_count // GROUPS
    grouped = Mesh(
        np.asarray(mesh.devices).reshape(dp_count, GROUPS, group_size), ("dp", "tg", "tj")
    )
    rows = ("dp",) + TENSOR
    return jax.shard_map(
        functools.partial(local, group_size=group_size, tensor_count=tensor_count),
        mesh=grouped,
        in_specs=(
            P(rows, None),
            P(rows, None),
            P(rows, None),
            P("dp", TENSOR),
            P("dp", None),
            P(None, TENSOR),
            P(TENSOR),
            P(),
            P(),
            P(TENSOR),
            P(TENSOR),
            P(TENSOR),
            P(),
            P(rows, None, None),
        ),
        out_specs=(
            P(rows, None),
            P(rows, None, None),
            P("dp", TENSOR),
            P("dp", TENSOR),
        ),
        check_vma=False,
    )
```

```python
import functools

import jax
import jax.numpy as jnp
from jax import lax
import numpy as np
from jax.sharding import Mesh, PartitionSpec as P

HEAD_DIM = 64
STATE = 256
GROUPS = 4
CONV_K = 4
INNER = 8192


EPSILON = 1e-05
TENSOR = ("tg", "tj")


def causal_conv(raw, state, weight, bias):
    length = raw.shape[0]
    padded = jnp.concatenate([state.astype(jnp.float32), raw.astype(jnp.float32)], axis=0)
    total = jnp.zeros(raw.shape, jnp.float32) + bias.astype(jnp.float32)[None, :]
    for kernel_tap in range(CONV_K):
        total = (
            total
            + weight[kernel_tap].astype(jnp.float32)[None, :]
            * padded[kernel_tap : kernel_tap + length]
        )
    return jax.nn.silu(total).astype(jnp.bfloat16)


def group_norm(mixed_y, norm_weight):
    rows = mixed_y.shape[0]
    values = mixed_y.astype(jnp.float32).reshape(rows, GROUPS, INNER // GROUPS)
    mean_square = jnp.mean(values * values, axis=2, keepdims=True)
    scaled = (values * lax.rsqrt(mean_square + EPSILON)).reshape(rows, INNER)
    return (scaled * norm_weight.astype(jnp.float32)[None, :]).astype(jnp.bfloat16)


def local(
    inner_x,
    inner_bc,
    step_raw,
    conv_state_x,
    conv_state_bc,
    conv_weight_x,
    conv_bias_x,
    conv_weight_bc,
    conv_bias_bc,
    step_bias,
    decay_rate,
    skip_gain,
    norm_weight,
    scan_state,
    *,
    group_size,
    tensor_count,
):
    device_rank = lax.axis_index("tg") * group_size + lax.axis_index("tj")
    token_rows = inner_x.shape[0]
    heads_here = step_bias.shape[0]
    x_width = heads_here * HEAD_DIM
    bc_width = inner_bc.shape[1] // tensor_count
    length = tensor_count * token_rows

    bc_send = jnp.transpose(inner_bc.reshape(token_rows, tensor_count, bc_width), (1, 0, 2))
    step_send = jnp.transpose(step_raw.reshape(token_rows, tensor_count, heads_here), (1, 0, 2))
    small_send = jnp.concatenate(
        [bc_send.reshape(tensor_count, -1), step_send.reshape(tensor_count, -1)], axis=1
    )
    small_recv = lax.all_to_all(small_send, TENSOR, 0, 0, tiled=True)
    bc_end = token_rows * bc_width
    head_bc_part = small_recv[:, :bc_end].reshape(length, bc_width)
    head_step = small_recv[:, bc_end:].reshape(length, heads_here)

    x_send = jnp.transpose(inner_x.reshape(token_rows, tensor_count, x_width), (1, 0, 2))
    x_recv = lax.all_to_all(x_send, TENSOR, 0, 0, tiled=True)
    head_x = x_recv.reshape(length, x_width)

    column_start = device_rank * bc_width
    own_state_bc = lax.dynamic_slice_in_dim(conv_state_bc, column_start, bc_width, 1)
    own_weight_bc = lax.dynamic_slice_in_dim(conv_weight_bc, column_start, bc_width, 1)
    own_bias_bc = lax.dynamic_slice_in_dim(conv_bias_bc, column_start, bc_width, 0)
    mixed_bc_part = causal_conv(head_bc_part, own_state_bc, own_weight_bc, own_bias_bc)
    group_rank = lax.axis_index("tj")
    across = lax.ppermute(
        mixed_bc_part, "tj", [(source, source ^ 2) for source in range(group_size)]
    )
    pair = jnp.stack([mixed_bc_part, across])
    beside = lax.ppermute(pair, "tj", [(source, source ^ 1) for source in range(group_size)])
    stacked = jnp.concatenate([pair, beside], axis=0)
    slot_of = jnp.array([0, 2, 1, 3], dtype=jnp.int32)
    order = slot_of[jnp.arange(group_size, dtype=jnp.int32) ^ group_rank]
    ordered = jnp.take(stacked, order, axis=0)
    mixed_bc = jnp.transpose(ordered, (1, 0, 2)).reshape(length, group_size * bc_width)
    input_map = mixed_bc[:, :STATE]
    output_map = mixed_bc[:, STATE:]

    step_size = jax.nn.softplus(head_step.astype(jnp.float32) + step_bias[None, :])
    running = jnp.cumsum(-step_size * decay_rate[None, :], axis=0)
    step_cols = jnp.transpose(step_size)
    running_cols = jnp.transpose(running)

    mixed_x = causal_conv(head_x, conv_state_x, conv_weight_x, conv_bias_x)
    values = mixed_x.reshape(length, heads_here, HEAD_DIM)
    values_t = jnp.transpose(values, (1, 2, 0))

    query_rows = min(256, length)
    pieces = []
    for row_start in range(0, length, query_rows):
        row_stop = row_start + query_rows
        scores = jnp.einsum(
            "tn,sn->ts",
            output_map[row_start:row_stop],
            input_map[:row_stop],
            preferred_element_type=jnp.float32,
        )
        causal = row_start + lax.broadcasted_iota(
            jnp.int32, (query_rows, row_stop), 0
        ) >= lax.broadcasted_iota(jnp.int32, (query_rows, row_stop), 1)
        log_gap = running_cols[:, row_start:row_stop, None] - running_cols[:, None, :row_stop]
        decayed = jnp.exp(jnp.where(causal[None], log_gap, 0.0))
        weights = jnp.where(
            causal[None], scores[None] * decayed * step_cols[:, None, :row_stop], 0.0
        ).astype(jnp.bfloat16)
        weights = lax.optimization_barrier(weights)
        pieces.append(
            jnp.einsum(
                "hts,hps->htp",
                weights,
                values_t[:, :, :row_stop],
                preferred_element_type=jnp.float32,
            )
        )
    local_all = jnp.concatenate(pieces, axis=1)
    carried = jnp.einsum(
        "tn,hpn->htp",
        output_map.astype(jnp.float32),
        scan_state,
        precision=lax.Precision.HIGHEST,
    )
    carried = carried * jnp.exp(running_cols)[:, :, None]
    channels = jnp.transpose(values_t, (0, 2, 1)).astype(jnp.float32)
    mixed = local_all + carried + skip_gain[:, None, None] * channels
    mixed_y = jnp.transpose(mixed.astype(jnp.bfloat16), (1, 0, 2)).reshape(length, x_width)
    tail_decay = jnp.exp(running[length - 1][None, :] - running) * step_size
    weighted = (input_map.astype(jnp.float32)[:, None, :] * tail_decay[:, :, None]).astype(
        jnp.bfloat16
    )
    gathered_in = jnp.einsum(
        "hps,shn->hpn", values_t, weighted, preferred_element_type=jnp.float32
    )
    final_state = jnp.exp(running[length - 1])[:, None, None] * scan_state + gathered_in

    token_y = lax.all_to_all(mixed_y, TENSOR, split_axis=0, concat_axis=1, tiled=True)
    normed = group_norm(token_y, norm_weight)
    tail_x = head_x[length - CONV_K + 1 :]
    tail_bc = head_bc_part[length - CONV_K + 1 :]
    return (normed, final_state, tail_x, tail_bc)


def solution(mesh):
    dp_count = mesh.shape["dp"]
    tensor_count = mesh.shape["tensor"]
    group_size = tensor_count // GROUPS
    grouped = Mesh(
        np.asarray(mesh.devices).reshape(dp_count, GROUPS, group_size), ("dp", "tg", "tj")
    )
    rows = ("dp",) + TENSOR
    return jax.shard_map(
        functools.partial(local, group_size=group_size, tensor_count=tensor_count),
        mesh=grouped,
        in_specs=(
            P(rows, None),
            P(rows, None),
            P(rows, None),
            P("dp", TENSOR),
            P("dp", None),
            P(None, TENSOR),
            P(TENSOR),
            P(),
            P(),
            P(TENSOR),
            P(TENSOR),
            P(TENSOR),
            P(),
            P(rows, None, None),
        ),
        out_specs=(
            P(rows, None),
            P(rows, None, None),
            P("dp", TENSOR),
            P("dp", TENSOR),
        ),
        check_vma=False,
    )
```

```python
import functools

import jax
import jax.numpy as jnp
from jax import lax
import numpy as np
from jax.sharding import Mesh, PartitionSpec as P

HEAD_DIM = 64
STATE = 256
GROUPS = 4
CONV_K = 4
INNER = 8192


EPSILON = 1e-05
TENSOR = ("tg", "tj")


def causal_conv(raw, state, weight, bias):
    length = raw.shape[0]
    padded = jnp.concatenate([state.astype(jnp.float32), raw.astype(jnp.float32)], axis=0)
    total = jnp.zeros(raw.shape, jnp.float32) + bias.astype(jnp.float32)[None, :]
    for kernel_tap in range(CONV_K):
        total = (
            total
            + weight[kernel_tap].astype(jnp.float32)[None, :]
            * padded[kernel_tap : kernel_tap + length]
        )
    return jax.nn.silu(total).astype(jnp.bfloat16)


def group_norm(mixed_y, norm_weight):
    rows = mixed_y.shape[0]
    values = mixed_y.astype(jnp.float32).reshape(rows, GROUPS, INNER // GROUPS)
    mean_square = jnp.mean(values * values, axis=2, keepdims=True)
    scaled = (values * lax.rsqrt(mean_square + EPSILON)).reshape(rows, INNER)
    return (scaled * norm_weight.astype(jnp.float32)[None, :]).astype(jnp.bfloat16)


def local(
    inner_x,
    inner_bc,
    step_raw,
    conv_state_x,
    conv_state_bc,
    conv_weight_x,
    conv_bias_x,
    conv_weight_bc,
    conv_bias_bc,
    step_bias,
    decay_rate,
    skip_gain,
    norm_weight,
    scan_state,
    *,
    group_size,
    tensor_count,
):
    device_rank = lax.axis_index("tg") * group_size + lax.axis_index("tj")
    token_rows = inner_x.shape[0]
    heads_here = step_bias.shape[0]
    x_width = heads_here * HEAD_DIM
    bc_width = inner_bc.shape[1] // tensor_count
    length = tensor_count * token_rows

    bc_send = jnp.transpose(inner_bc.reshape(token_rows, tensor_count, bc_width), (1, 0, 2))
    step_send = jnp.transpose(step_raw.reshape(token_rows, tensor_count, heads_here), (1, 0, 2))
    small_send = jnp.concatenate(
        [bc_send.reshape(tensor_count, -1), step_send.reshape(tensor_count, -1)], axis=1
    )
    small_recv = lax.all_to_all(small_send, TENSOR, 0, 0, tiled=True)
    bc_end = token_rows * bc_width
    head_bc_part = small_recv[:, :bc_end].reshape(length, bc_width)
    head_step = small_recv[:, bc_end:].reshape(length, heads_here)

    column_start = device_rank * bc_width
    own_state_bc = lax.dynamic_slice_in_dim(conv_state_bc, column_start, bc_width, 1)
    own_weight_bc = lax.dynamic_slice_in_dim(conv_weight_bc, column_start, bc_width, 1)
    own_bias_bc = lax.dynamic_slice_in_dim(conv_bias_bc, column_start, bc_width, 0)
    mixed_bc_part = causal_conv(head_bc_part, own_state_bc, own_weight_bc, own_bias_bc)
    group_rank = lax.axis_index("tj")
    across = lax.ppermute(
        mixed_bc_part, "tj", [(source, source ^ 2) for source in range(group_size)]
    )
    pair = jnp.stack([mixed_bc_part, across])
    beside = lax.ppermute(pair, "tj", [(source, source ^ 1) for source in range(group_size)])
    stacked = jnp.concatenate([pair, beside], axis=0)
    slot_of = jnp.array([0, 2, 1, 3], dtype=jnp.int32)
    order = slot_of[jnp.arange(group_size, dtype=jnp.int32) ^ group_rank]
    ordered = jnp.take(stacked, order, axis=0)
    mixed_bc = jnp.transpose(ordered, (1, 0, 2)).reshape(length, group_size * bc_width)
    x_send = jnp.transpose(inner_x.reshape(token_rows, tensor_count, x_width), (1, 0, 2))
    x_send, mixed_bc = lax.optimization_barrier((x_send, mixed_bc))
    x_recv = lax.all_to_all(x_send, TENSOR, 0, 0, tiled=True)
    head_x = x_recv.reshape(length, x_width)
    input_map = mixed_bc[:, :STATE]
    output_map = mixed_bc[:, STATE:]

    step_size = jax.nn.softplus(head_step.astype(jnp.float32) + step_bias[None, :])
    running = jnp.cumsum(-step_size * decay_rate[None, :], axis=0)
    step_cols = jnp.transpose(step_size)
    running_cols = jnp.transpose(running)

    mixed_x = causal_conv(head_x, conv_state_x, conv_weight_x, conv_bias_x)
    values = mixed_x.reshape(length, heads_here, HEAD_DIM)
    values_t = jnp.transpose(values, (1, 2, 0))

    query_rows = min(256, length)
    pieces = []
    for row_start in range(0, length, query_rows):
        row_stop = row_start + query_rows
        scores = jnp.einsum(
            "tn,sn->ts",
            output_map[row_start:row_stop],
            input_map[:row_stop],
            preferred_element_type=jnp.float32,
        )
        causal = row_start + lax.broadcasted_iota(
            jnp.int32, (query_rows, row_stop), 0
        ) >= lax.broadcasted_iota(jnp.int32, (query_rows, row_stop), 1)
        log_gap = running_cols[:, row_start:row_stop, None] - running_cols[:, None, :row_stop]
        decayed = jnp.exp(jnp.where(causal[None], log_gap, 0.0))
        weights = jnp.where(
            causal[None], scores[None] * decayed * step_cols[:, None, :row_stop], 0.0
        ).astype(jnp.bfloat16)
        weights = lax.optimization_barrier(weights)
        pieces.append(
            jnp.einsum(
                "hts,hps->htp",
                weights,
                values_t[:, :, :row_stop],
                preferred_element_type=jnp.float32,
            )
        )
    local_all = jnp.concatenate(pieces, axis=1)
    carried = jnp.einsum(
        "tn,hpn->htp",
        output_map.astype(jnp.float32),
        scan_state,
        precision=lax.Precision.HIGHEST,
    )
    carried = carried * jnp.exp(running_cols)[:, :, None]
    channels = jnp.transpose(values_t, (0, 2, 1)).astype(jnp.float32)
    mixed = local_all + carried + skip_gain[:, None, None] * channels
    mixed_y = jnp.transpose(mixed.astype(jnp.bfloat16), (1, 0, 2)).reshape(length, x_width)
    tail_decay = jnp.exp(running[length - 1][None, :] - running) * step_size
    weighted = (input_map.astype(jnp.float32)[:, None, :] * tail_decay[:, :, None]).astype(
        jnp.bfloat16
    )
    gathered_in = jnp.einsum(
        "hps,shn->hpn", values_t, weighted, preferred_element_type=jnp.float32
    )
    final_state = jnp.exp(running[length - 1])[:, None, None] * scan_state + gathered_in

    token_y = lax.all_to_all(mixed_y, TENSOR, split_axis=0, concat_axis=1, tiled=True)
    normed = group_norm(token_y, norm_weight)
    tail_x = head_x[length - CONV_K + 1 :]
    tail_bc = head_bc_part[length - CONV_K + 1 :]
    return (normed, final_state, tail_x, tail_bc)


def solution(mesh):
    dp_count = mesh.shape["dp"]
    tensor_count = mesh.shape["tensor"]
    group_size = tensor_count // GROUPS
    grouped = Mesh(
        np.asarray(mesh.devices).reshape(dp_count, GROUPS, group_size), ("dp", "tg", "tj")
    )
    rows = ("dp",) + TENSOR
    return jax.shard_map(
        functools.partial(local, group_size=group_size, tensor_count=tensor_count),
        mesh=grouped,
        in_specs=(
            P(rows, None),
            P(rows, None),
            P(rows, None),
            P("dp", TENSOR),
            P("dp", None),
            P(None, TENSOR),
            P(TENSOR),
            P(),
            P(),
            P(TENSOR),
            P(TENSOR),
            P(TENSOR),
            P(),
            P(rows, None, None),
        ),
        out_specs=(
            P(rows, None),
            P(rows, None, None),
            P("dp", TENSOR),
            P("dp", TENSOR),
        ),
        check_vma=False,
    )
```

```python
import functools

import jax
import jax.numpy as jnp
from jax import lax
import numpy as np
from jax.sharding import Mesh, PartitionSpec as P

HEAD_DIM = 64
STATE = 256
GROUPS = 4
CONV_K = 4
INNER = 8192


EPSILON = 1e-05
TENSOR = ("tg", "tj")


def causal_conv(raw, state, weight, bias):
    length = raw.shape[0]
    padded = jnp.concatenate([state.astype(jnp.float32), raw.astype(jnp.float32)], axis=0)
    total = jnp.zeros(raw.shape, jnp.float32) + bias.astype(jnp.float32)[None, :]
    for kernel_tap in range(CONV_K):
        total = (
            total
            + weight[kernel_tap].astype(jnp.float32)[None, :]
            * padded[kernel_tap : kernel_tap + length]
        )
    return jax.nn.silu(total).astype(jnp.bfloat16)


def group_norm(mixed_y, norm_weight):
    rows = mixed_y.shape[0]
    values = mixed_y.astype(jnp.float32).reshape(rows, GROUPS, INNER // GROUPS)
    mean_square = jnp.mean(values * values, axis=2, keepdims=True)
    scaled = (values * lax.rsqrt(mean_square + EPSILON)).reshape(rows, INNER)
    return (scaled * norm_weight.astype(jnp.float32)[None, :]).astype(jnp.bfloat16)


def local(
    inner_x,
    inner_bc,
    step_raw,
    conv_state_x,
    conv_state_bc,
    conv_weight_x,
    conv_bias_x,
    conv_weight_bc,
    conv_bias_bc,
    step_bias,
    decay_rate,
    skip_gain,
    norm_weight,
    scan_state,
    *,
    group_size,
    tensor_count,
):
    device_rank = lax.axis_index("tg") * group_size + lax.axis_index("tj")
    token_rows = inner_x.shape[0]
    heads_here = step_bias.shape[0]
    x_width = heads_here * HEAD_DIM
    bc_width = inner_bc.shape[1] // tensor_count
    length = tensor_count * token_rows

    quarters = inner_bc.reshape(token_rows, GROUPS, 2, group_size // 2, bc_width)
    across_quarters = jnp.flip(quarters, axis=2)
    bc_send = jnp.stack([quarters, across_quarters], axis=4).reshape(
        token_rows, tensor_count, 2, bc_width
    )
    bc_send = jnp.transpose(bc_send, (1, 0, 2, 3))
    x_send = jnp.transpose(inner_x.reshape(token_rows, tensor_count, x_width), (1, 0, 2))
    step_send = jnp.transpose(step_raw.reshape(token_rows, tensor_count, heads_here), (1, 0, 2))
    send = jnp.concatenate(
        [
            x_send.reshape(tensor_count, -1),
            bc_send.reshape(tensor_count, -1),
            step_send.reshape(tensor_count, -1),
        ],
        axis=1,
    )
    recv = lax.all_to_all(send, TENSOR, 0, 0, tiled=True)
    x_end = token_rows * x_width
    bc_end = x_end + token_rows * 2 * bc_width
    head_x = recv[:, :x_end].reshape(length, x_width)
    head_bc_pair = recv[:, x_end:bc_end].reshape(length, 2 * bc_width)
    head_step = recv[:, bc_end:].reshape(length, heads_here)

    group_rank = lax.axis_index("tj")
    column_start = device_rank * bc_width
    across_start = (device_rank ^ 2) * bc_width
    pair_state_bc = jnp.concatenate(
        [
            lax.dynamic_slice_in_dim(conv_state_bc, column_start, bc_width, 1),
            lax.dynamic_slice_in_dim(conv_state_bc, across_start, bc_width, 1),
        ],
        axis=1,
    )
    pair_weight_bc = jnp.concatenate(
        [
            lax.dynamic_slice_in_dim(conv_weight_bc, column_start, bc_width, 1),
            lax.dynamic_slice_in_dim(conv_weight_bc, across_start, bc_width, 1),
        ],
        axis=1,
    )
    pair_bias_bc = jnp.concatenate(
        [
            lax.dynamic_slice_in_dim(conv_bias_bc, column_start, bc_width, 0),
            lax.dynamic_slice_in_dim(conv_bias_bc, across_start, bc_width, 0),
        ],
        axis=0,
    )
    mixed_pair = causal_conv(head_bc_pair, pair_state_bc, pair_weight_bc, pair_bias_bc)
    pair = jnp.transpose(mixed_pair.reshape(length, 2, bc_width), (1, 0, 2))
    beside = lax.ppermute(pair, "tj", [(source, source ^ 1) for source in range(group_size)])
    stacked = jnp.concatenate([pair, beside], axis=0)
    slot_of = jnp.array([0, 2, 1, 3], dtype=jnp.int32)
    order = slot_of[jnp.arange(group_size, dtype=jnp.int32) ^ group_rank]
    ordered = jnp.take(stacked, order, axis=0)
    mixed_bc = jnp.transpose(ordered, (1, 0, 2)).reshape(length, group_size * bc_width)
    input_map = mixed_bc[:, :STATE]
    output_map = mixed_bc[:, STATE:]

    step_size = jax.nn.softplus(head_step.astype(jnp.float32) + step_bias[None, :])
    running = jnp.cumsum(-step_size * decay_rate[None, :], axis=0)
    step_cols = jnp.transpose(step_size)
    running_cols = jnp.transpose(running)

    mixed_x = causal_conv(head_x, conv_state_x, conv_weight_x, conv_bias_x)
    values = mixed_x.reshape(length, heads_here, HEAD_DIM)
    values_t = jnp.transpose(values, (1, 2, 0))

    query_rows = min(256, length)
    pieces = []
    for row_start in range(0, length, query_rows):
        row_stop = row_start + query_rows
        scores = jnp.einsum(
            "tn,sn->ts",
            output_map[row_start:row_stop],
            input_map[:row_stop],
            preferred_element_type=jnp.float32,
        )
        causal = row_start + lax.broadcasted_iota(
            jnp.int32, (query_rows, row_stop), 0
        ) >= lax.broadcasted_iota(jnp.int32, (query_rows, row_stop), 1)
        log_gap = running_cols[:, row_start:row_stop, None] - running_cols[:, None, :row_stop]
        decayed = jnp.exp(jnp.where(causal[None], log_gap, 0.0))
        weights = jnp.where(
            causal[None], scores[None] * decayed * step_cols[:, None, :row_stop], 0.0
        ).astype(jnp.bfloat16)
        weights = lax.optimization_barrier(weights)
        pieces.append(
            jnp.einsum(
                "hts,hps->htp",
                weights,
                values_t[:, :, :row_stop],
                preferred_element_type=jnp.float32,
            )
        )
    local_all = jnp.concatenate(pieces, axis=1)
    carried = jnp.einsum(
        "tn,hpn->htp",
        output_map.astype(jnp.float32),
        scan_state,
        precision=lax.Precision.HIGHEST,
    )
    carried = carried * jnp.exp(running_cols)[:, :, None]
    channels = jnp.transpose(values_t, (0, 2, 1)).astype(jnp.float32)
    mixed = local_all + carried + skip_gain[:, None, None] * channels
    mixed_y = jnp.transpose(mixed.astype(jnp.bfloat16), (1, 0, 2)).reshape(length, x_width)
    tail_decay = jnp.exp(running[length - 1][None, :] - running) * step_size
    weighted = (input_map.astype(jnp.float32)[:, None, :] * tail_decay[:, :, None]).astype(
        jnp.bfloat16
    )
    gathered_in = jnp.einsum(
        "hps,shn->hpn", values_t, weighted, preferred_element_type=jnp.float32
    )
    final_state = jnp.exp(running[length - 1])[:, None, None] * scan_state + gathered_in

    token_y = lax.all_to_all(mixed_y, TENSOR, split_axis=0, concat_axis=1, tiled=True)
    normed = group_norm(token_y, norm_weight)
    tail_x = head_x[length - CONV_K + 1 :]
    tail_bc = head_bc_pair[length - CONV_K + 1 :, :bc_width]
    return (normed, final_state, tail_x, tail_bc)


def solution(mesh):
    dp_count = mesh.shape["dp"]
    tensor_count = mesh.shape["tensor"]
    group_size = tensor_count // GROUPS
    grouped = Mesh(
        np.asarray(mesh.devices).reshape(dp_count, GROUPS, group_size), ("dp", "tg", "tj")
    )
    rows = ("dp",) + TENSOR
    return jax.shard_map(
        functools.partial(local, group_size=group_size, tensor_count=tensor_count),
        mesh=grouped,
        in_specs=(
            P(rows, None),
            P(rows, None),
            P(rows, None),
            P("dp", TENSOR),
            P("dp", None),
            P(None, TENSOR),
            P(TENSOR),
            P(),
            P(),
            P(TENSOR),
            P(TENSOR),
            P(TENSOR),
            P(),
            P(rows, None, None),
        ),
        out_specs=(
            P(rows, None),
            P(rows, None, None),
            P("dp", TENSOR),
            P("dp", TENSOR),
        ),
        check_vma=False,
    )
```

```python
import functools

import jax
import jax.numpy as jnp
from jax import lax
import numpy as np
from jax.sharding import Mesh, PartitionSpec as P

HEAD_DIM = 64
STATE = 256
GROUPS = 4
CONV_K = 4
INNER = 8192


EPSILON = 1e-05
TENSOR = ("tg", "tj")


def causal_conv(raw, state, weight, bias):
    length = raw.shape[0]
    padded = jnp.concatenate([state.astype(jnp.float32), raw.astype(jnp.float32)], axis=0)
    total = jnp.zeros(raw.shape, jnp.float32) + bias.astype(jnp.float32)[None, :]
    for kernel_tap in range(CONV_K):
        total = (
            total
            + weight[kernel_tap].astype(jnp.float32)[None, :]
            * padded[kernel_tap : kernel_tap + length]
        )
    return jax.nn.silu(total).astype(jnp.bfloat16)


def group_norm(mixed_y, norm_weight):
    rows = mixed_y.shape[0]
    values = mixed_y.astype(jnp.float32).reshape(rows, GROUPS, INNER // GROUPS)
    mean_square = jnp.mean(values * values, axis=2, keepdims=True)
    scaled = (values * lax.rsqrt(mean_square + EPSILON)).reshape(rows, INNER)
    return (scaled * norm_weight.astype(jnp.float32)[None, :]).astype(jnp.bfloat16)


def local(
    inner_x,
    inner_bc,
    step_raw,
    conv_state_x,
    conv_state_bc,
    conv_weight_x,
    conv_bias_x,
    conv_weight_bc,
    conv_bias_bc,
    step_bias,
    decay_rate,
    skip_gain,
    norm_weight,
    scan_state,
    *,
    group_size,
    tensor_count,
):
    device_rank = lax.axis_index("tg") * group_size + lax.axis_index("tj")
    token_rows = inner_x.shape[0]
    heads_here = step_bias.shape[0]
    x_width = heads_here * HEAD_DIM
    bc_width = inner_bc.shape[1] // tensor_count
    length = tensor_count * token_rows

    x_send = jnp.transpose(inner_x.reshape(token_rows, tensor_count, x_width), (1, 0, 2))
    x_recv = lax.all_to_all(x_send, TENSOR, 0, 0, tiled=True)
    head_x = x_recv.reshape(length, x_width)

    quarters = inner_bc.reshape(token_rows, GROUPS, 2, group_size // 2, bc_width)
    across_quarters = jnp.flip(quarters, axis=2)
    bc_send = jnp.stack([quarters, across_quarters], axis=4).reshape(
        token_rows, tensor_count, 2 * bc_width
    )
    bc_send = jnp.transpose(bc_send, (1, 0, 2))
    step_send = jnp.transpose(step_raw.reshape(token_rows, tensor_count, heads_here), (1, 0, 2))
    small_send = jnp.concatenate(
        [bc_send.reshape(tensor_count, -1), step_send.reshape(tensor_count, -1)], axis=1
    )
    slots = [lax.dynamic_index_in_dim(small_send, device_rank, 0, keepdims=False)]
    for shift in range(1, tensor_count):
        target = (device_rank + shift) % tensor_count
        slots.append(
            lax.ppermute(
                lax.dynamic_index_in_dim(small_send, target, 0, keepdims=False),
                TENSOR,
                [(source, (source + shift) % tensor_count) for source in range(tensor_count)],
            )
        )
    arrived = jnp.stack(slots)
    by_source = (device_rank - jnp.arange(tensor_count, dtype=jnp.int32)) % tensor_count
    small_recv = jnp.take(arrived, by_source, axis=0)
    bc_end = token_rows * 2 * bc_width
    head_bc_pair = small_recv[:, :bc_end].reshape(length, 2 * bc_width)
    head_step = small_recv[:, bc_end:].reshape(length, heads_here)

    group_rank = lax.axis_index("tj")
    column_start = device_rank * bc_width
    across_start = (device_rank ^ 2) * bc_width
    pair_state_bc = jnp.concatenate(
        [
            lax.dynamic_slice_in_dim(conv_state_bc, column_start, bc_width, 1),
            lax.dynamic_slice_in_dim(conv_state_bc, across_start, bc_width, 1),
        ],
        axis=1,
    )
    pair_weight_bc = jnp.concatenate(
        [
            lax.dynamic_slice_in_dim(conv_weight_bc, column_start, bc_width, 1),
            lax.dynamic_slice_in_dim(conv_weight_bc, across_start, bc_width, 1),
        ],
        axis=1,
    )
    pair_bias_bc = jnp.concatenate(
        [
            lax.dynamic_slice_in_dim(conv_bias_bc, column_start, bc_width, 0),
            lax.dynamic_slice_in_dim(conv_bias_bc, across_start, bc_width, 0),
        ],
        axis=0,
    )
    mixed_pair = causal_conv(head_bc_pair, pair_state_bc, pair_weight_bc, pair_bias_bc)
    pair = jnp.transpose(mixed_pair.reshape(length, 2, bc_width), (1, 0, 2))
    beside = lax.ppermute(pair, "tj", [(source, source ^ 1) for source in range(group_size)])
    stacked = jnp.concatenate([pair, beside], axis=0)
    slot_of = jnp.array([0, 2, 1, 3], dtype=jnp.int32)
    order = slot_of[jnp.arange(group_size, dtype=jnp.int32) ^ group_rank]
    ordered = jnp.take(stacked, order, axis=0)
    mixed_bc = jnp.transpose(ordered, (1, 0, 2)).reshape(length, group_size * bc_width)
    input_map = mixed_bc[:, :STATE]
    output_map = mixed_bc[:, STATE:]

    step_size = jax.nn.softplus(head_step.astype(jnp.float32) + step_bias[None, :])
    running = jnp.cumsum(-step_size * decay_rate[None, :], axis=0)
    step_cols = jnp.transpose(step_size)
    running_cols = jnp.transpose(running)

    mixed_x = causal_conv(head_x, conv_state_x, conv_weight_x, conv_bias_x)
    values = mixed_x.reshape(length, heads_here, HEAD_DIM)
    values_t = jnp.transpose(values, (1, 2, 0))

    query_rows = min(256, length)
    pieces = []
    for row_start in range(0, length, query_rows):
        row_stop = row_start + query_rows
        scores = jnp.einsum(
            "tn,sn->ts",
            output_map[row_start:row_stop],
            input_map[:row_stop],
            preferred_element_type=jnp.float32,
        )
        causal = row_start + lax.broadcasted_iota(
            jnp.int32, (query_rows, row_stop), 0
        ) >= lax.broadcasted_iota(jnp.int32, (query_rows, row_stop), 1)
        log_gap = running_cols[:, row_start:row_stop, None] - running_cols[:, None, :row_stop]
        decayed = jnp.exp(jnp.where(causal[None], log_gap, 0.0))
        weights = jnp.where(
            causal[None], scores[None] * decayed * step_cols[:, None, :row_stop], 0.0
        ).astype(jnp.bfloat16)
        weights = lax.optimization_barrier(weights)
        pieces.append(
            jnp.einsum(
                "hts,hps->htp",
                weights,
                values_t[:, :, :row_stop],
                preferred_element_type=jnp.float32,
            )
        )
    local_all = jnp.concatenate(pieces, axis=1)
    carried = jnp.einsum(
        "tn,hpn->htp",
        output_map.astype(jnp.float32),
        scan_state,
        precision=lax.Precision.HIGHEST,
    )
    carried = carried * jnp.exp(running_cols)[:, :, None]
    channels = jnp.transpose(values_t, (0, 2, 1)).astype(jnp.float32)
    mixed = local_all + carried + skip_gain[:, None, None] * channels
    mixed_y = jnp.transpose(mixed.astype(jnp.bfloat16), (1, 0, 2)).reshape(length, x_width)
    tail_decay = jnp.exp(running[length - 1][None, :] - running) * step_size
    weighted = (input_map.astype(jnp.float32)[:, None, :] * tail_decay[:, :, None]).astype(
        jnp.bfloat16
    )
    gathered_in = jnp.einsum(
        "hps,shn->hpn", values_t, weighted, preferred_element_type=jnp.float32
    )
    final_state = jnp.exp(running[length - 1])[:, None, None] * scan_state + gathered_in

    token_y = lax.all_to_all(mixed_y, TENSOR, split_axis=0, concat_axis=1, tiled=True)
    normed = group_norm(token_y, norm_weight)
    tail_x = head_x[length - CONV_K + 1 :]
    tail_bc = head_bc_pair[length - CONV_K + 1 :, :bc_width]
    return (normed, final_state, tail_x, tail_bc)


def solution(mesh):
    dp_count = mesh.shape["dp"]
    tensor_count = mesh.shape["tensor"]
    group_size = tensor_count // GROUPS
    grouped = Mesh(
        np.asarray(mesh.devices).reshape(dp_count, GROUPS, group_size), ("dp", "tg", "tj")
    )
    rows = ("dp",) + TENSOR
    return jax.shard_map(
        functools.partial(local, group_size=group_size, tensor_count=tensor_count),
        mesh=grouped,
        in_specs=(
            P(rows, None),
            P(rows, None),
            P(rows, None),
            P("dp", TENSOR),
            P("dp", None),
            P(None, TENSOR),
            P(TENSOR),
            P(),
            P(),
            P(TENSOR),
            P(TENSOR),
            P(TENSOR),
            P(),
            P(rows, None, None),
        ),
        out_specs=(
            P(rows, None),
            P(rows, None, None),
            P("dp", TENSOR),
            P("dp", TENSOR),
        ),
        check_vma=False,
    )
```

```python
import functools

import jax
import jax.numpy as jnp
from jax import lax
import numpy as np
from jax.sharding import Mesh, PartitionSpec as P

HEAD_DIM = 64
STATE = 256
GROUPS = 4
CONV_K = 4
INNER = 8192


EPSILON = 1e-05
TENSOR = ("tg", "tj")


def causal_conv(raw, state, weight, bias):
    length = raw.shape[0]
    padded = jnp.concatenate([state.astype(jnp.float32), raw.astype(jnp.float32)], axis=0)
    total = jnp.zeros(raw.shape, jnp.float32) + bias.astype(jnp.float32)[None, :]
    for kernel_tap in range(CONV_K):
        total = (
            total
            + weight[kernel_tap].astype(jnp.float32)[None, :]
            * padded[kernel_tap : kernel_tap + length]
        )
    return jax.nn.silu(total).astype(jnp.bfloat16)


def group_norm(mixed_y, norm_weight):
    rows = mixed_y.shape[0]
    values = mixed_y.astype(jnp.float32).reshape(rows, GROUPS, INNER // GROUPS)
    mean_square = jnp.mean(values * values, axis=2, keepdims=True)
    scaled = (values * lax.rsqrt(mean_square + EPSILON)).reshape(rows, INNER)
    return (scaled * norm_weight.astype(jnp.float32)[None, :]).astype(jnp.bfloat16)


def local(
    inner_x,
    inner_bc,
    step_raw,
    conv_state_x,
    conv_state_bc,
    conv_weight_x,
    conv_bias_x,
    conv_weight_bc,
    conv_bias_bc,
    step_bias,
    decay_rate,
    skip_gain,
    norm_weight,
    scan_state,
    *,
    group_size,
    tensor_count,
):
    device_rank = lax.axis_index("tg") * group_size + lax.axis_index("tj")
    token_rows = inner_x.shape[0]
    heads_here = step_bias.shape[0]
    x_width = heads_here * HEAD_DIM
    bc_width = inner_bc.shape[1] // tensor_count
    length = tensor_count * token_rows

    quarters = inner_bc.reshape(token_rows, GROUPS, 2, group_size // 2, bc_width)
    across_quarters = jnp.flip(quarters, axis=2)
    bc_send = jnp.stack([quarters, across_quarters], axis=4).reshape(
        token_rows, tensor_count, 2 * bc_width
    )
    bc_send = jnp.transpose(bc_send, (1, 0, 2))
    step_send = jnp.transpose(step_raw.reshape(token_rows, tensor_count, heads_here), (1, 0, 2))
    small_send = jnp.concatenate(
        [bc_send.reshape(tensor_count, -1), step_send.reshape(tensor_count, -1)], axis=1
    )
    small_recv = lax.all_to_all(small_send, TENSOR, 0, 0, tiled=True)
    bc_end = token_rows * 2 * bc_width
    head_bc_pair = small_recv[:, :bc_end].reshape(length, 2 * bc_width)
    head_step = small_recv[:, bc_end:].reshape(length, heads_here)

    x_send = jnp.transpose(inner_x.reshape(token_rows, tensor_count, x_width), (1, 0, 2))
    x_recv = lax.all_to_all(x_send, TENSOR, 0, 0, tiled=True)
    head_x = x_recv.reshape(length, x_width)

    group_rank = lax.axis_index("tj")
    column_start = device_rank * bc_width
    across_start = (device_rank ^ 2) * bc_width
    pair_state_bc = jnp.concatenate(
        [
            lax.dynamic_slice_in_dim(conv_state_bc, column_start, bc_width, 1),
            lax.dynamic_slice_in_dim(conv_state_bc, across_start, bc_width, 1),
        ],
        axis=1,
    )
    pair_weight_bc = jnp.concatenate(
        [
            lax.dynamic_slice_in_dim(conv_weight_bc, column_start, bc_width, 1),
            lax.dynamic_slice_in_dim(conv_weight_bc, across_start, bc_width, 1),
        ],
        axis=1,
    )
    pair_bias_bc = jnp.concatenate(
        [
            lax.dynamic_slice_in_dim(conv_bias_bc, column_start, bc_width, 0),
            lax.dynamic_slice_in_dim(conv_bias_bc, across_start, bc_width, 0),
        ],
        axis=0,
    )
    mixed_pair = causal_conv(head_bc_pair, pair_state_bc, pair_weight_bc, pair_bias_bc)
    pair = jnp.transpose(mixed_pair.reshape(length, 2, bc_width), (1, 0, 2))
    beside = lax.ppermute(pair, "tj", [(source, source ^ 1) for source in range(group_size)])
    stacked = jnp.concatenate([pair, beside], axis=0)
    slot_of = jnp.array([0, 2, 1, 3], dtype=jnp.int32)
    order = slot_of[jnp.arange(group_size, dtype=jnp.int32) ^ group_rank]
    ordered = jnp.take(stacked, order, axis=0)
    mixed_bc = jnp.transpose(ordered, (1, 0, 2)).reshape(length, group_size * bc_width)
    input_map = mixed_bc[:, :STATE]
    output_map = mixed_bc[:, STATE:]

    step_size = jax.nn.softplus(head_step.astype(jnp.float32) + step_bias[None, :])
    running = jnp.cumsum(-step_size * decay_rate[None, :], axis=0)
    step_cols = jnp.transpose(step_size)
    running_cols = jnp.transpose(running)

    mixed_x = causal_conv(head_x, conv_state_x, conv_weight_x, conv_bias_x)
    values = mixed_x.reshape(length, heads_here, HEAD_DIM)
    values_t = jnp.transpose(values, (1, 2, 0))

    query_rows = min(256, length)
    pieces = []
    for row_start in range(0, length, query_rows):
        row_stop = row_start + query_rows
        scores = jnp.einsum(
            "tn,sn->ts",
            output_map[row_start:row_stop],
            input_map[:row_stop],
            preferred_element_type=jnp.float32,
        )
        causal = row_start + lax.broadcasted_iota(
            jnp.int32, (query_rows, row_stop), 0
        ) >= lax.broadcasted_iota(jnp.int32, (query_rows, row_stop), 1)
        log_gap = running_cols[:, row_start:row_stop, None] - running_cols[:, None, :row_stop]
        decayed = jnp.exp(jnp.where(causal[None], log_gap, 0.0))
        weights = jnp.where(
            causal[None], scores[None] * decayed * step_cols[:, None, :row_stop], 0.0
        ).astype(jnp.bfloat16)
        weights = lax.optimization_barrier(weights)
        pieces.append(
            jnp.einsum(
                "hts,hps->htp",
                weights,
                values_t[:, :, :row_stop],
                preferred_element_type=jnp.float32,
            )
        )
    local_all = jnp.concatenate(pieces, axis=1)
    carried = jnp.einsum(
        "tn,hpn->htp",
        output_map.astype(jnp.float32),
        scan_state,
        precision=lax.Precision.HIGHEST,
    )
    carried = carried * jnp.exp(running_cols)[:, :, None]
    channels = jnp.transpose(values_t, (0, 2, 1)).astype(jnp.float32)
    mixed = local_all + carried + skip_gain[:, None, None] * channels
    mixed_y = jnp.transpose(mixed.astype(jnp.bfloat16), (1, 0, 2)).reshape(length, x_width)
    tail_decay = jnp.exp(running[length - 1][None, :] - running) * step_size
    weighted = (input_map.astype(jnp.float32)[:, None, :] * tail_decay[:, :, None]).astype(
        jnp.bfloat16
    )
    gathered_in = jnp.einsum(
        "hps,shn->hpn", values_t, weighted, preferred_element_type=jnp.float32
    )
    final_state = jnp.exp(running[length - 1])[:, None, None] * scan_state + gathered_in

    token_y = lax.all_to_all(mixed_y, TENSOR, split_axis=0, concat_axis=1, tiled=True)
    normed = group_norm(token_y, norm_weight)
    tail_x = head_x[length - CONV_K + 1 :]
    tail_bc = head_bc_pair[length - CONV_K + 1 :, :bc_width]
    return (normed, final_state, tail_x, tail_bc)


def solution(mesh):
    dp_count = mesh.shape["dp"]
    tensor_count = mesh.shape["tensor"]
    group_size = tensor_count // GROUPS
    grouped = Mesh(
        np.asarray(mesh.devices).reshape(dp_count, GROUPS, group_size), ("dp", "tg", "tj")
    )
    rows = ("dp",) + TENSOR
    return jax.shard_map(
        functools.partial(local, group_size=group_size, tensor_count=tensor_count),
        mesh=grouped,
        in_specs=(
            P(rows, None),
            P(rows, None),
            P(rows, None),
            P("dp", TENSOR),
            P("dp", None),
            P(None, TENSOR),
            P(TENSOR),
            P(),
            P(),
            P(TENSOR),
            P(TENSOR),
            P(TENSOR),
            P(),
            P(rows, None, None),
        ),
        out_specs=(
            P(rows, None),
            P(rows, None, None),
            P("dp", TENSOR),
            P("dp", TENSOR),
        ),
        check_vma=False,
    )
```

```python
import functools

import jax
import jax.numpy as jnp
from jax import lax
import numpy as np
from jax.sharding import Mesh, PartitionSpec as P

HEAD_DIM = 64
STATE = 256
GROUPS = 4
CONV_K = 4
INNER = 8192


EPSILON = 1e-05
TENSOR = ("tg", "tj")


def causal_conv(raw, state, weight, bias):
    length = raw.shape[0]
    padded = jnp.concatenate([state.astype(jnp.float32), raw.astype(jnp.float32)], axis=0)
    total = jnp.zeros(raw.shape, jnp.float32) + bias.astype(jnp.float32)[None, :]
    for kernel_tap in range(CONV_K):
        total = (
            total
            + weight[kernel_tap].astype(jnp.float32)[None, :]
            * padded[kernel_tap : kernel_tap + length]
        )
    return jax.nn.silu(total).astype(jnp.bfloat16)


def group_norm(mixed_y, norm_weight):
    rows = mixed_y.shape[0]
    values = mixed_y.astype(jnp.float32).reshape(rows, GROUPS, INNER // GROUPS)
    mean_square = jnp.mean(values * values, axis=2, keepdims=True)
    scaled = (values * lax.rsqrt(mean_square + EPSILON)).reshape(rows, INNER)
    return (scaled * norm_weight.astype(jnp.float32)[None, :]).astype(jnp.bfloat16)


def local(
    inner_x,
    inner_bc,
    step_raw,
    conv_state_x,
    conv_state_bc,
    conv_weight_x,
    conv_bias_x,
    conv_weight_bc,
    conv_bias_bc,
    step_bias,
    decay_rate,
    skip_gain,
    norm_weight,
    scan_state,
    *,
    group_size,
    tensor_count,
):
    device_rank = lax.axis_index("tg") * group_size + lax.axis_index("tj")
    token_rows = inner_x.shape[0]
    heads_here = step_bias.shape[0]
    x_width = heads_here * HEAD_DIM
    bc_width = inner_bc.shape[1] // tensor_count
    length = tensor_count * token_rows

    quarters = inner_bc.reshape(token_rows, GROUPS, 2, group_size // 2, bc_width)
    across_quarters = jnp.flip(quarters, axis=2)
    bc_send = jnp.stack([quarters, across_quarters], axis=4).reshape(
        token_rows, tensor_count, 2 * bc_width
    )
    bc_send = jnp.transpose(bc_send, (1, 0, 2))
    step_send = jnp.transpose(step_raw.reshape(token_rows, tensor_count, heads_here), (1, 0, 2))
    x_send = jnp.transpose(inner_x.reshape(token_rows, tensor_count, x_width), (1, 0, 2))
    half_width = x_width // 2
    half_heads = heads_here // 2
    small_send = jnp.concatenate(
        [
            bc_send.reshape(tensor_count, -1),
            step_send.reshape(tensor_count, -1),
            x_send[:, :, :half_width].reshape(tensor_count, -1),
        ],
        axis=1,
    )
    small_recv = lax.all_to_all(small_send, TENSOR, 0, 0, tiled=True)
    late_send, small_recv = lax.optimization_barrier((x_send[:, :, half_width:], small_recv))
    bc_end = token_rows * 2 * bc_width
    step_end = bc_end + token_rows * heads_here
    head_bc_pair = small_recv[:, :bc_end].reshape(length, 2 * bc_width)
    head_step = small_recv[:, bc_end:step_end].reshape(length, heads_here)
    early_x = small_recv[:, step_end:].reshape(length, half_width)

    late_recv = lax.all_to_all(late_send, TENSOR, 0, 0, tiled=True)
    late_x = late_recv.reshape(length, half_width)

    group_rank = lax.axis_index("tj")
    column_start = device_rank * bc_width
    across_start = (device_rank ^ 2) * bc_width
    pair_state_bc = jnp.concatenate(
        [
            lax.dynamic_slice_in_dim(conv_state_bc, column_start, bc_width, 1),
            lax.dynamic_slice_in_dim(conv_state_bc, across_start, bc_width, 1),
        ],
        axis=1,
    )
    pair_weight_bc = jnp.concatenate(
        [
            lax.dynamic_slice_in_dim(conv_weight_bc, column_start, bc_width, 1),
            lax.dynamic_slice_in_dim(conv_weight_bc, across_start, bc_width, 1),
        ],
        axis=1,
    )
    pair_bias_bc = jnp.concatenate(
        [
            lax.dynamic_slice_in_dim(conv_bias_bc, column_start, bc_width, 0),
            lax.dynamic_slice_in_dim(conv_bias_bc, across_start, bc_width, 0),
        ],
        axis=0,
    )
    mixed_pair = causal_conv(head_bc_pair, pair_state_bc, pair_weight_bc, pair_bias_bc)
    pair = jnp.transpose(mixed_pair.reshape(length, 2, bc_width), (1, 0, 2))
    beside = lax.ppermute(pair, "tj", [(source, source ^ 1) for source in range(group_size)])
    stacked = jnp.concatenate([pair, beside], axis=0)
    slot_of = jnp.array([0, 2, 1, 3], dtype=jnp.int32)
    order = slot_of[jnp.arange(group_size, dtype=jnp.int32) ^ group_rank]
    ordered = jnp.take(stacked, order, axis=0)
    mixed_bc = jnp.transpose(ordered, (1, 0, 2)).reshape(length, group_size * bc_width)
    input_map = mixed_bc[:, :STATE]
    output_map = mixed_bc[:, STATE:]

    step_size = jax.nn.softplus(head_step.astype(jnp.float32) + step_bias[None, :])
    running = jnp.cumsum(-step_size * decay_rate[None, :], axis=0)
    step_cols = jnp.transpose(step_size)
    running_cols = jnp.transpose(running)

    early_values_t = jnp.transpose(
        causal_conv(
            early_x,
            conv_state_x[:, :half_width],
            conv_weight_x[:, :half_width],
            conv_bias_x[:half_width],
        ).reshape(length, half_heads, HEAD_DIM),
        (1, 2, 0),
    )
    late_values_t = jnp.transpose(
        causal_conv(
            late_x,
            conv_state_x[:, half_width:],
            conv_weight_x[:, half_width:],
            conv_bias_x[half_width:],
        ).reshape(length, half_heads, HEAD_DIM),
        (1, 2, 0),
    )

    query_rows = min(256, length)
    early_pieces = []
    late_pieces = []
    for row_start in range(0, length, query_rows):
        row_stop = row_start + query_rows
        scores = jnp.einsum(
            "tn,sn->ts",
            output_map[row_start:row_stop],
            input_map[:row_stop],
            preferred_element_type=jnp.float32,
        )
        causal = row_start + lax.broadcasted_iota(
            jnp.int32, (query_rows, row_stop), 0
        ) >= lax.broadcasted_iota(jnp.int32, (query_rows, row_stop), 1)
        log_gap = running_cols[:, row_start:row_stop, None] - running_cols[:, None, :row_stop]
        decayed = jnp.exp(jnp.where(causal[None], log_gap, 0.0))
        weights = jnp.where(
            causal[None], scores[None] * decayed * step_cols[:, None, :row_stop], 0.0
        ).astype(jnp.bfloat16)
        weights = lax.optimization_barrier(weights)
        early_pieces.append(
            jnp.einsum(
                "hts,hps->htp",
                weights[:half_heads],
                early_values_t[:, :, :row_stop],
                preferred_element_type=jnp.float32,
            )
        )
        late_pieces.append(
            jnp.einsum(
                "hts,hps->htp",
                weights[half_heads:],
                late_values_t[:, :, :row_stop],
                preferred_element_type=jnp.float32,
            )
        )
    carried = jnp.einsum(
        "tn,hpn->htp",
        output_map.astype(jnp.float32),
        scan_state,
        precision=lax.Precision.HIGHEST,
    )
    carried = carried * jnp.exp(running_cols)[:, :, None]
    early_mixed = (
        jnp.concatenate(early_pieces, axis=1)
        + carried[:half_heads]
        + skip_gain[:half_heads, None, None]
        * jnp.transpose(early_values_t, (0, 2, 1)).astype(jnp.float32)
    )
    late_mixed = (
        jnp.concatenate(late_pieces, axis=1)
        + carried[half_heads:]
        + skip_gain[half_heads:, None, None]
        * jnp.transpose(late_values_t, (0, 2, 1)).astype(jnp.float32)
    )
    mixed = jnp.concatenate([early_mixed, late_mixed], axis=0)
    values_t = jnp.concatenate([early_values_t, late_values_t], axis=0)
    mixed_y = jnp.transpose(mixed.astype(jnp.bfloat16), (1, 0, 2)).reshape(length, x_width)
    tail_decay = jnp.exp(running[length - 1][None, :] - running) * step_size
    weighted = (input_map.astype(jnp.float32)[:, None, :] * tail_decay[:, :, None]).astype(
        jnp.bfloat16
    )
    gathered_in = jnp.einsum(
        "hps,shn->hpn", values_t, weighted, preferred_element_type=jnp.float32
    )
    final_state = jnp.exp(running[length - 1])[:, None, None] * scan_state + gathered_in

    token_y = lax.all_to_all(mixed_y, TENSOR, split_axis=0, concat_axis=1, tiled=True)
    normed = group_norm(token_y, norm_weight)
    tail_x = jnp.concatenate(
        [early_x[length - CONV_K + 1 :], late_x[length - CONV_K + 1 :]], axis=1
    )
    tail_bc = head_bc_pair[length - CONV_K + 1 :, :bc_width]
    return (normed, final_state, tail_x, tail_bc)


def solution(mesh):
    dp_count = mesh.shape["dp"]
    tensor_count = mesh.shape["tensor"]
    group_size = tensor_count // GROUPS
    grouped = Mesh(
        np.asarray(mesh.devices).reshape(dp_count, GROUPS, group_size), ("dp", "tg", "tj")
    )
    rows = ("dp",) + TENSOR
    return jax.shard_map(
        functools.partial(local, group_size=group_size, tensor_count=tensor_count),
        mesh=grouped,
        in_specs=(
            P(rows, None),
            P(rows, None),
            P(rows, None),
            P("dp", TENSOR),
            P("dp", None),
            P(None, TENSOR),
            P(TENSOR),
            P(),
            P(),
            P(TENSOR),
            P(TENSOR),
            P(TENSOR),
            P(),
            P(rows, None, None),
        ),
        out_specs=(
            P(rows, None),
            P(rows, None, None),
            P("dp", TENSOR),
            P("dp", TENSOR),
        ),
        check_vma=False,
    )
```

```python
import functools

import jax
import jax.numpy as jnp
from jax import lax
import numpy as np
from jax.sharding import Mesh, PartitionSpec as P

HEAD_DIM = 64
STATE = 256
GROUPS = 4
CONV_K = 4
INNER = 8192


EPSILON = 1e-05
TENSOR = ("tg", "tj")


def causal_conv(raw, state, weight, bias):
    length = raw.shape[0]
    padded = jnp.concatenate([state.astype(jnp.float32), raw.astype(jnp.float32)], axis=0)
    total = jnp.zeros(raw.shape, jnp.float32) + bias.astype(jnp.float32)[None, :]
    for kernel_tap in range(CONV_K):
        total = (
            total
            + weight[kernel_tap].astype(jnp.float32)[None, :]
            * padded[kernel_tap : kernel_tap + length]
        )
    return jax.nn.silu(total).astype(jnp.bfloat16)


def group_norm(mixed_y, norm_weight):
    rows = mixed_y.shape[0]
    values = mixed_y.astype(jnp.float32).reshape(rows, GROUPS, INNER // GROUPS)
    mean_square = jnp.mean(values * values, axis=2, keepdims=True)
    scaled = (values * lax.rsqrt(mean_square + EPSILON)).reshape(rows, INNER)
    return (scaled * norm_weight.astype(jnp.float32)[None, :]).astype(jnp.bfloat16)


def local(
    inner_x,
    inner_bc,
    step_raw,
    conv_state_x,
    conv_state_bc,
    conv_weight_x,
    conv_bias_x,
    conv_weight_bc,
    conv_bias_bc,
    step_bias,
    decay_rate,
    skip_gain,
    norm_weight,
    scan_state,
    *,
    group_size,
    tensor_count,
):
    device_rank = lax.axis_index("tg") * group_size + lax.axis_index("tj")
    token_rows = inner_x.shape[0]
    heads_here = step_bias.shape[0]
    x_width = heads_here * HEAD_DIM
    bc_width = inner_bc.shape[1] // tensor_count
    length = tensor_count * token_rows

    quarters = inner_bc.reshape(token_rows, GROUPS, 2, group_size // 2, bc_width)
    across_quarters = jnp.flip(quarters, axis=2)
    bc_rows = jnp.transpose(
        jnp.stack([quarters, across_quarters], axis=4), (1, 2, 3, 0, 4, 5)
    ).reshape(tensor_count, token_rows * 2, bc_width)
    step_rows = jnp.transpose(
        step_raw.reshape(token_rows, tensor_count, heads_here), (1, 0, 2)
    ).reshape(tensor_count, token_rows * heads_here // bc_width, bc_width)
    small_send = jnp.concatenate([bc_rows, step_rows], axis=1)
    small_recv = lax.all_to_all(small_send, TENSOR, 0, 0, tiled=True)
    bc_rows_end = token_rows * 2
    head_bc_pair = small_recv[:, :bc_rows_end].reshape(length, 2 * bc_width)
    head_step = small_recv[:, bc_rows_end:].reshape(length, heads_here)

    x_send = jnp.transpose(inner_x.reshape(token_rows, tensor_count, x_width), (1, 0, 2))
    x_recv = lax.all_to_all(x_send, TENSOR, 0, 0, tiled=True)
    head_x = x_recv.reshape(length, x_width)

    group_rank = lax.axis_index("tj")
    column_start = device_rank * bc_width
    across_start = (device_rank ^ 2) * bc_width
    pair_state_bc = jnp.concatenate(
        [
            lax.dynamic_slice_in_dim(conv_state_bc, column_start, bc_width, 1),
            lax.dynamic_slice_in_dim(conv_state_bc, across_start, bc_width, 1),
        ],
        axis=1,
    )
    pair_weight_bc = jnp.concatenate(
        [
            lax.dynamic_slice_in_dim(conv_weight_bc, column_start, bc_width, 1),
            lax.dynamic_slice_in_dim(conv_weight_bc, across_start, bc_width, 1),
        ],
        axis=1,
    )
    pair_bias_bc = jnp.concatenate(
        [
            lax.dynamic_slice_in_dim(conv_bias_bc, column_start, bc_width, 0),
            lax.dynamic_slice_in_dim(conv_bias_bc, across_start, bc_width, 0),
        ],
        axis=0,
    )
    mixed_pair = causal_conv(head_bc_pair, pair_state_bc, pair_weight_bc, pair_bias_bc)
    pair = jnp.transpose(mixed_pair.reshape(length, 2, bc_width), (1, 0, 2))
    beside = lax.ppermute(pair, "tj", [(source, source ^ 1) for source in range(group_size)])
    stacked = jnp.concatenate([pair, beside], axis=0)
    slot_of = jnp.array([0, 2, 1, 3], dtype=jnp.int32)
    order = slot_of[jnp.arange(group_size, dtype=jnp.int32) ^ group_rank]
    ordered = jnp.take(stacked, order, axis=0)
    mixed_bc = jnp.transpose(ordered, (1, 0, 2)).reshape(length, group_size * bc_width)
    input_map = mixed_bc[:, :STATE]
    output_map = mixed_bc[:, STATE:]

    step_size = jax.nn.softplus(head_step.astype(jnp.float32) + step_bias[None, :])
    running = jnp.cumsum(-step_size * decay_rate[None, :], axis=0)
    step_cols = jnp.transpose(step_size)
    running_cols = jnp.transpose(running)

    mixed_x = causal_conv(head_x, conv_state_x, conv_weight_x, conv_bias_x)
    values = mixed_x.reshape(length, heads_here, HEAD_DIM)
    values_t = jnp.transpose(values, (1, 2, 0))

    query_rows = min(256, length)
    pieces = []
    for row_start in range(0, length, query_rows):
        row_stop = row_start + query_rows
        scores = jnp.einsum(
            "tn,sn->ts",
            output_map[row_start:row_stop],
            input_map[:row_stop],
            preferred_element_type=jnp.float32,
        )
        causal = row_start + lax.broadcasted_iota(
            jnp.int32, (query_rows, row_stop), 0
        ) >= lax.broadcasted_iota(jnp.int32, (query_rows, row_stop), 1)
        log_gap = running_cols[:, row_start:row_stop, None] - running_cols[:, None, :row_stop]
        decayed = jnp.exp(jnp.where(causal[None], log_gap, 0.0))
        weights = jnp.where(
            causal[None], scores[None] * decayed * step_cols[:, None, :row_stop], 0.0
        ).astype(jnp.bfloat16)
        weights = lax.optimization_barrier(weights)
        pieces.append(
            jnp.einsum(
                "hts,hps->htp",
                weights,
                values_t[:, :, :row_stop],
                preferred_element_type=jnp.float32,
            )
        )
    local_all = jnp.concatenate(pieces, axis=1)
    carried = jnp.einsum(
        "tn,hpn->htp",
        output_map.astype(jnp.float32),
        scan_state,
        precision=lax.Precision.HIGHEST,
    )
    carried = carried * jnp.exp(running_cols)[:, :, None]
    channels = jnp.transpose(values_t, (0, 2, 1)).astype(jnp.float32)
    mixed = local_all + carried + skip_gain[:, None, None] * channels
    mixed_y = jnp.transpose(mixed.astype(jnp.bfloat16), (1, 0, 2)).reshape(length, x_width)
    tail_decay = jnp.exp(running[length - 1][None, :] - running) * step_size
    weighted = (input_map.astype(jnp.float32)[:, None, :] * tail_decay[:, :, None]).astype(
        jnp.bfloat16
    )
    gathered_in = jnp.einsum(
        "hps,shn->hpn", values_t, weighted, preferred_element_type=jnp.float32
    )
    final_state = jnp.exp(running[length - 1])[:, None, None] * scan_state + gathered_in

    token_y = lax.all_to_all(mixed_y, TENSOR, split_axis=0, concat_axis=1, tiled=True)
    normed = group_norm(token_y, norm_weight)
    tail_x = head_x[length - CONV_K + 1 :]
    tail_bc = head_bc_pair[length - CONV_K + 1 :, :bc_width]
    return (normed, final_state, tail_x, tail_bc)


def solution(mesh):
    dp_count = mesh.shape["dp"]
    tensor_count = mesh.shape["tensor"]
    group_size = tensor_count // GROUPS
    grouped = Mesh(
        np.asarray(mesh.devices).reshape(dp_count, GROUPS, group_size), ("dp", "tg", "tj")
    )
    rows = ("dp",) + TENSOR
    return jax.shard_map(
        functools.partial(local, group_size=group_size, tensor_count=tensor_count),
        mesh=grouped,
        in_specs=(
            P(rows, None),
            P(rows, None),
            P(rows, None),
            P("dp", TENSOR),
            P("dp", None),
            P(None, TENSOR),
            P(TENSOR),
            P(),
            P(),
            P(TENSOR),
            P(TENSOR),
            P(TENSOR),
            P(),
            P(rows, None, None),
        ),
        out_specs=(
            P(rows, None),
            P(rows, None, None),
            P("dp", TENSOR),
            P("dp", TENSOR),
        ),
        check_vma=False,
    )
```

```python
import functools

import jax
import jax.numpy as jnp
from jax import lax
import numpy as np
from jax.sharding import Mesh, PartitionSpec as P

HEAD_DIM = 64
STATE = 256
GROUPS = 4
CONV_K = 4
INNER = 8192


EPSILON = 1e-05
TENSOR = ("tg", "tj")


def causal_conv(raw, state, weight, bias):
    length = raw.shape[0]
    padded = jnp.concatenate([state.astype(jnp.float32), raw.astype(jnp.float32)], axis=0)
    total = jnp.zeros(raw.shape, jnp.float32) + bias.astype(jnp.float32)[None, :]
    for kernel_tap in range(CONV_K):
        total = (
            total
            + weight[kernel_tap].astype(jnp.float32)[None, :]
            * padded[kernel_tap : kernel_tap + length]
        )
    return jax.nn.silu(total).astype(jnp.bfloat16)


def group_norm(mixed_y, norm_weight):
    rows = mixed_y.shape[0]
    values = mixed_y.astype(jnp.float32).reshape(rows, GROUPS, INNER // GROUPS)
    mean_square = jnp.mean(values * values, axis=2, keepdims=True)
    scaled = (values * lax.rsqrt(mean_square + EPSILON)).reshape(rows, INNER)
    return (scaled * norm_weight.astype(jnp.float32)[None, :]).astype(jnp.bfloat16)


def local(
    inner_x,
    inner_bc,
    step_raw,
    conv_state_x,
    conv_state_bc,
    conv_weight_x,
    conv_bias_x,
    conv_weight_bc,
    conv_bias_bc,
    step_bias,
    decay_rate,
    skip_gain,
    norm_weight,
    scan_state,
    *,
    group_size,
    tensor_count,
):
    device_rank = lax.axis_index("tg") * group_size + lax.axis_index("tj")
    token_rows = inner_x.shape[0]
    heads_here = step_bias.shape[0]
    x_width = heads_here * HEAD_DIM
    bc_width = inner_bc.shape[1] // tensor_count
    length = tensor_count * token_rows

    quarters = jnp.transpose(
        inner_bc.reshape(token_rows, GROUPS, 2, group_size // 2, bc_width), (1, 3, 0, 2, 4)
    )
    bc_rows = jnp.broadcast_to(
        quarters[:, None], (GROUPS, 2) + quarters.shape[1:]
    ).reshape(tensor_count, token_rows * 2, bc_width)
    step_rows = jnp.transpose(
        step_raw.reshape(token_rows, tensor_count, heads_here), (1, 0, 2)
    ).reshape(tensor_count, token_rows * heads_here // bc_width, bc_width)
    small_send = jnp.concatenate([bc_rows, step_rows], axis=1)
    small_recv = lax.all_to_all(small_send, TENSOR, 0, 0, tiled=True)
    bc_rows_end = token_rows * 2
    head_bc_pair = small_recv[:, :bc_rows_end].reshape(length, 2 * bc_width)
    head_step = small_recv[:, bc_rows_end:].reshape(length, heads_here)

    x_send = jnp.transpose(inner_x.reshape(token_rows, tensor_count, x_width), (1, 0, 2))
    x_recv = lax.all_to_all(x_send, TENSOR, 0, 0, tiled=True)
    head_x = x_recv.reshape(length, x_width)

    group_rank = lax.axis_index("tj")
    high_bit = (group_rank // 2) % 2
    low_bit = group_rank % 2
    column_start = (device_rank - 2 * high_bit) * bc_width
    across_start = (device_rank - 2 * high_bit + 2) * bc_width
    pair_state_bc = jnp.concatenate(
        [
            lax.dynamic_slice_in_dim(conv_state_bc, column_start, bc_width, 1),
            lax.dynamic_slice_in_dim(conv_state_bc, across_start, bc_width, 1),
        ],
        axis=1,
    )
    pair_weight_bc = jnp.concatenate(
        [
            lax.dynamic_slice_in_dim(conv_weight_bc, column_start, bc_width, 1),
            lax.dynamic_slice_in_dim(conv_weight_bc, across_start, bc_width, 1),
        ],
        axis=1,
    )
    pair_bias_bc = jnp.concatenate(
        [
            lax.dynamic_slice_in_dim(conv_bias_bc, column_start, bc_width, 0),
            lax.dynamic_slice_in_dim(conv_bias_bc, across_start, bc_width, 0),
        ],
        axis=0,
    )
    mixed_pair = causal_conv(head_bc_pair, pair_state_bc, pair_weight_bc, pair_bias_bc)
    pair = jnp.transpose(mixed_pair.reshape(length, 2, bc_width), (1, 0, 2))
    beside = lax.ppermute(pair, "tj", [(source, source ^ 1) for source in range(group_size)])
    stacked = jnp.concatenate([pair, beside], axis=0)
    slot_of = jnp.array([0, 2, 1, 3], dtype=jnp.int32)
    order = slot_of[jnp.arange(group_size, dtype=jnp.int32) ^ low_bit]
    ordered = jnp.take(stacked, order, axis=0)
    mixed_bc = jnp.transpose(ordered, (1, 0, 2)).reshape(length, group_size * bc_width)
    input_map = mixed_bc[:, :STATE]
    output_map = mixed_bc[:, STATE:]

    step_size = jax.nn.softplus(head_step.astype(jnp.float32) + step_bias[None, :])
    running = jnp.cumsum(-step_size * decay_rate[None, :], axis=0)
    step_cols = jnp.transpose(step_size)
    running_cols = jnp.transpose(running)

    mixed_x = causal_conv(head_x, conv_state_x, conv_weight_x, conv_bias_x)
    values = mixed_x.reshape(length, heads_here, HEAD_DIM)
    values_t = jnp.transpose(values, (1, 2, 0))

    query_rows = min(256, length)
    pieces = []
    for row_start in range(0, length, query_rows):
        row_stop = row_start + query_rows
        scores = jnp.einsum(
            "tn,sn->ts",
            output_map[row_start:row_stop],
            input_map[:row_stop],
            preferred_element_type=jnp.float32,
        )
        causal = row_start + lax.broadcasted_iota(
            jnp.int32, (query_rows, row_stop), 0
        ) >= lax.broadcasted_iota(jnp.int32, (query_rows, row_stop), 1)
        log_gap = running_cols[:, row_start:row_stop, None] - running_cols[:, None, :row_stop]
        decayed = jnp.exp(jnp.where(causal[None], log_gap, 0.0))
        weights = jnp.where(
            causal[None], scores[None] * decayed * step_cols[:, None, :row_stop], 0.0
        ).astype(jnp.bfloat16)
        weights = lax.optimization_barrier(weights)
        pieces.append(
            jnp.einsum(
                "hts,hps->htp",
                weights,
                values_t[:, :, :row_stop],
                preferred_element_type=jnp.float32,
            )
        )
    local_all = jnp.concatenate(pieces, axis=1)
    carried = jnp.einsum(
        "tn,hpn->htp",
        output_map.astype(jnp.float32),
        scan_state,
        precision=lax.Precision.HIGHEST,
    )
    carried = carried * jnp.exp(running_cols)[:, :, None]
    channels = jnp.transpose(values_t, (0, 2, 1)).astype(jnp.float32)
    mixed = local_all + carried + skip_gain[:, None, None] * channels
    mixed_y = jnp.transpose(mixed.astype(jnp.bfloat16), (1, 0, 2)).reshape(length, x_width)
    tail_decay = jnp.exp(running[length - 1][None, :] - running) * step_size
    weighted = (input_map.astype(jnp.float32)[:, None, :] * tail_decay[:, :, None]).astype(
        jnp.bfloat16
    )
    gathered_in = jnp.einsum(
        "hps,shn->hpn", values_t, weighted, preferred_element_type=jnp.float32
    )
    final_state = jnp.exp(running[length - 1])[:, None, None] * scan_state + gathered_in

    token_y = lax.all_to_all(mixed_y, TENSOR, split_axis=0, concat_axis=1, tiled=True)
    normed = group_norm(token_y, norm_weight)
    tail_x = head_x[length - CONV_K + 1 :]
    tail_bc = lax.dynamic_slice_in_dim(
        head_bc_pair[length - CONV_K + 1 :], high_bit * bc_width, bc_width, 1
    )
    return (normed, final_state, tail_x, tail_bc)


def solution(mesh):
    dp_count = mesh.shape["dp"]
    tensor_count = mesh.shape["tensor"]
    group_size = tensor_count // GROUPS
    grouped = Mesh(
        np.asarray(mesh.devices).reshape(dp_count, GROUPS, group_size), ("dp", "tg", "tj")
    )
    rows = ("dp",) + TENSOR
    return jax.shard_map(
        functools.partial(local, group_size=group_size, tensor_count=tensor_count),
        mesh=grouped,
        in_specs=(
            P(rows, None),
            P(rows, None),
            P(rows, None),
            P("dp", TENSOR),
            P("dp", None),
            P(None, TENSOR),
            P(TENSOR),
            P(),
            P(),
            P(TENSOR),
            P(TENSOR),
            P(TENSOR),
            P(),
            P(rows, None, None),
        ),
        out_specs=(
            P(rows, None),
            P(rows, None, None),
            P("dp", TENSOR),
            P("dp", TENSOR),
        ),
        check_vma=False,
    )
```

```python
import functools

import jax
import jax.numpy as jnp
from jax import lax
import numpy as np
from jax.sharding import Mesh, PartitionSpec as P

HEAD_DIM = 64
STATE = 256
GROUPS = 4
CONV_K = 4
INNER = 8192


EPSILON = 1e-05
TENSOR = ("tg", "tj")


def causal_conv(raw, state, weight, bias):
    length = raw.shape[0]
    padded = jnp.concatenate([state.astype(jnp.float32), raw.astype(jnp.float32)], axis=0)
    total = jnp.zeros(raw.shape, jnp.float32) + bias.astype(jnp.float32)[None, :]
    for kernel_tap in range(CONV_K):
        total = (
            total
            + weight[kernel_tap].astype(jnp.float32)[None, :]
            * padded[kernel_tap : kernel_tap + length]
        )
    return jax.nn.silu(total).astype(jnp.bfloat16)


def group_norm(mixed_y, norm_weight):
    rows = mixed_y.shape[0]
    values = mixed_y.astype(jnp.float32).reshape(rows, GROUPS, INNER // GROUPS)
    mean_square = jnp.mean(values * values, axis=2, keepdims=True)
    scaled = (values * lax.rsqrt(mean_square + EPSILON)).reshape(rows, INNER)
    return (scaled * norm_weight.astype(jnp.float32)[None, :]).astype(jnp.bfloat16)


def local(
    inner_x,
    inner_bc,
    step_raw,
    conv_state_x,
    conv_state_bc,
    conv_weight_x,
    conv_bias_x,
    conv_weight_bc,
    conv_bias_bc,
    step_bias,
    decay_rate,
    skip_gain,
    norm_weight,
    scan_state,
    *,
    group_size,
    tensor_count,
):
    device_rank = lax.axis_index("tg") * group_size + lax.axis_index("tj")
    token_rows = inner_x.shape[0]
    heads_here = step_bias.shape[0]
    x_width = heads_here * HEAD_DIM
    bc_width = inner_bc.shape[1] // tensor_count
    length = tensor_count * token_rows

    quarters = jnp.transpose(
        inner_bc.reshape(token_rows, GROUPS, 2, group_size // 2, bc_width), (1, 3, 0, 2, 4)
    )
    bc_rows = jnp.broadcast_to(
        quarters[:, None], (GROUPS, 2) + quarters.shape[1:]
    ).reshape(tensor_count, token_rows * 2, bc_width)
    step_rows = jnp.transpose(
        step_raw.reshape(token_rows, tensor_count, heads_here), (1, 0, 2)
    ).reshape(tensor_count, token_rows * heads_here // bc_width, bc_width)
    small_send = jnp.concatenate([bc_rows, step_rows], axis=1)
    small_recv = lax.all_to_all(small_send, TENSOR, 0, 0, tiled=True)
    bc_rows_end = token_rows * 2
    head_bc_pair = small_recv[:, :bc_rows_end].reshape(length, 2 * bc_width)
    head_step = small_recv[:, bc_rows_end:].reshape(length, heads_here)

    x_send = jnp.transpose(inner_x.reshape(token_rows, tensor_count, x_width), (1, 0, 2))
    x_recv = lax.all_to_all(x_send, TENSOR, 0, 0, tiled=True)
    head_x = x_recv.reshape(length, x_width)

    group_rank = lax.axis_index("tj")
    high_bit = (group_rank // 2) % 2
    low_bit = group_rank % 2
    column_start = (device_rank - 2 * high_bit) * bc_width
    across_start = (device_rank - 2 * high_bit + 2) * bc_width
    pair_state_bc = jnp.concatenate(
        [
            lax.dynamic_slice_in_dim(conv_state_bc, column_start, bc_width, 1),
            lax.dynamic_slice_in_dim(conv_state_bc, across_start, bc_width, 1),
        ],
        axis=1,
    )
    pair_weight_bc = jnp.concatenate(
        [
            lax.dynamic_slice_in_dim(conv_weight_bc, column_start, bc_width, 1),
            lax.dynamic_slice_in_dim(conv_weight_bc, across_start, bc_width, 1),
        ],
        axis=1,
    )
    pair_bias_bc = jnp.concatenate(
        [
            lax.dynamic_slice_in_dim(conv_bias_bc, column_start, bc_width, 0),
            lax.dynamic_slice_in_dim(conv_bias_bc, across_start, bc_width, 0),
        ],
        axis=0,
    )
    mixed_pair = causal_conv(head_bc_pair, pair_state_bc, pair_weight_bc, pair_bias_bc)
    pair = jnp.transpose(mixed_pair.reshape(length, 2, bc_width), (1, 0, 2))
    beside = lax.ppermute(pair, "tj", [(source, source ^ 1) for source in range(group_size)])
    stacked = jnp.concatenate([pair, beside], axis=0)
    slot_of = jnp.array([0, 2, 1, 3], dtype=jnp.int32)
    order = slot_of[jnp.arange(group_size, dtype=jnp.int32) ^ low_bit]
    ordered = jnp.take(stacked, order, axis=0)
    mixed_bc = jnp.transpose(ordered, (1, 0, 2)).reshape(length, group_size * bc_width)
    input_map = mixed_bc[:, :STATE]
    output_map = mixed_bc[:, STATE:]

    step_size = jax.nn.softplus(head_step.astype(jnp.float32) + step_bias[None, :])
    running = jnp.cumsum(-step_size * decay_rate[None, :], axis=0)
    step_cols = jnp.transpose(step_size)
    running_cols = jnp.transpose(running)

    mixed_x = causal_conv(head_x, conv_state_x, conv_weight_x, conv_bias_x)
    values = mixed_x.reshape(length, heads_here, HEAD_DIM)
    values_t = jnp.transpose(values, (1, 2, 0))

    query_rows = min(128, length)
    pieces = []
    for row_start in range(0, length, query_rows):
        row_stop = row_start + query_rows
        scores = jnp.einsum(
            "tn,sn->ts",
            output_map[row_start:row_stop],
            input_map[:row_stop],
            preferred_element_type=jnp.float32,
        )
        causal = row_start + lax.broadcasted_iota(
            jnp.int32, (query_rows, row_stop), 0
        ) >= lax.broadcasted_iota(jnp.int32, (query_rows, row_stop), 1)
        log_gap = running_cols[:, row_start:row_stop, None] - running_cols[:, None, :row_stop]
        decayed = jnp.exp(jnp.where(causal[None], log_gap, 0.0))
        weights = jnp.where(
            causal[None], scores[None] * decayed * step_cols[:, None, :row_stop], 0.0
        ).astype(jnp.bfloat16)
        weights = lax.optimization_barrier(weights)
        pieces.append(
            jnp.einsum(
                "hts,hps->htp",
                weights,
                values_t[:, :, :row_stop],
                preferred_element_type=jnp.float32,
            )
        )
    local_all = jnp.concatenate(pieces, axis=1)
    carried = jnp.einsum(
        "tn,hpn->htp",
        output_map.astype(jnp.float32),
        scan_state,
        precision=lax.Precision.HIGHEST,
    )
    carried = carried * jnp.exp(running_cols)[:, :, None]
    channels = jnp.transpose(values_t, (0, 2, 1)).astype(jnp.float32)
    mixed = local_all + carried + skip_gain[:, None, None] * channels
    mixed_y = jnp.transpose(mixed.astype(jnp.bfloat16), (1, 0, 2)).reshape(length, x_width)
    tail_decay = jnp.exp(running[length - 1][None, :] - running) * step_size
    weighted = (input_map.astype(jnp.float32)[:, None, :] * tail_decay[:, :, None]).astype(
        jnp.bfloat16
    )
    gathered_in = jnp.einsum(
        "hps,shn->hpn", values_t, weighted, preferred_element_type=jnp.float32
    )
    final_state = jnp.exp(running[length - 1])[:, None, None] * scan_state + gathered_in

    token_y = lax.all_to_all(mixed_y, TENSOR, split_axis=0, concat_axis=1, tiled=True)
    normed = group_norm(token_y, norm_weight)
    tail_x = head_x[length - CONV_K + 1 :]
    tail_bc = lax.dynamic_slice_in_dim(
        head_bc_pair[length - CONV_K + 1 :], high_bit * bc_width, bc_width, 1
    )
    return (normed, final_state, tail_x, tail_bc)


def solution(mesh):
    dp_count = mesh.shape["dp"]
    tensor_count = mesh.shape["tensor"]
    group_size = tensor_count // GROUPS
    grouped = Mesh(
        np.asarray(mesh.devices).reshape(dp_count, GROUPS, group_size), ("dp", "tg", "tj")
    )
    rows = ("dp",) + TENSOR
    return jax.shard_map(
        functools.partial(local, group_size=group_size, tensor_count=tensor_count),
        mesh=grouped,
        in_specs=(
            P(rows, None),
            P(rows, None),
            P(rows, None),
            P("dp", TENSOR),
            P("dp", None),
            P(None, TENSOR),
            P(TENSOR),
            P(),
            P(),
            P(TENSOR),
            P(TENSOR),
            P(TENSOR),
            P(),
            P(rows, None, None),
        ),
        out_specs=(
            P(rows, None),
            P(rows, None, None),
            P("dp", TENSOR),
            P("dp", TENSOR),
        ),
        check_vma=False,
    )
```
